128 devices in a mesh: section: 2 (over y_lo), row: 8 (over x, core), col: 8 (over z, y_hi).
Axes of the slice: x: 4, y: 4 (y_hi: 2, y_lo: 2; y = y_hi * 2 + y_lo), z: 4, core: 2. Of those that a mesh axis runs over, the one named last changes fastest.
Arguments:
- features: bfloat16 [2, 192, 64, 1024], P(None, None, 'row', 'col'), may hold values from -36 to 36
- labels: int32 [2, 64, 1024], P(None, 'row', 'col'), may hold values from 0 to 15
- dw_weight: float32 [192, 49], replicated, may hold values from -0.875 to 0.875
- dw_bias: float32 [192], replicated, may hold values from -3 to 3
- norm_gain: float32 [192], replicated, may hold values from 0.25 to 1.75
- norm_bias: float32 [192], replicated, may hold values from -2 to 2
- w_in: bfloat16 [192, 768], replicated, may hold values from -0.4375 to 0.4375
- b_in: float32 [768], replicated, may hold values from -3 to 3
- w_out: bfloat16 [768, 192], replicated, may hold values from -0.21875 to 0.21875
- b_out: float32 [192], replicated, may hold values from -3 to 3
- layer_scale: float32 [192], replicated, may hold values from 0.2 to 1
- w_lateral: bfloat16 [192, 512], replicated, may hold values from -0.4375 to 0.4375
- b_lateral: float32 [512], replicated, may hold values from -3 to 3
- w_class: bfloat16 [512, 16], replicated, may hold values from -1.8 to 1.8
- b_class: float32 [16], replicated, may hold values from -4 to 4
Outputs:
- d_features: float32 [2, 192, 64, 1024], P('section', None, 'row', 'col')
- loss: float32 [], replicated
- grad_dw_weight: float32 [192, 49], replicated
- grad_dw_bias: float32 [192], replicated
- grad_norm_gain: float32 [192], replicated
- grad_norm_bias: float32 [192], replicated
- grad_w_in: float32 [192, 768], replicated
- grad_b_in: float32 [768], replicated
- grad_w_out: float32 [768, 192], replicated
- grad_b_out: float32 [192], replicated
- grad_layer_scale: float32 [192], replicated
- grad_w_lateral: float32 [192, 512], replicated
- grad_b_lateral: float32 [512], replicated
- grad_w_class: float32 [512, 16], replicated
- grad_b_class: float32 [16], replicated
The draws below stay inside these ranges and needn't reach their ends.
All inputs are finite; a program needn't handle non-finite values.
Results may differ from the reference program's by a relative error of at most 0.0059.
Values may be sent and summed in bfloat16 or wider, within the bound.
No kernel may reach another device: no remote copies, remote signals or barrier semaphores. Data moves between devices by JAX's collectives and lax.ppermute only.
A program may use at most 128 MiB of HBM per device.

```python
import math
import jax
import jax.numpy as jnp
from jax import lax

C = 192
HID = 768
LAT = 512
CLASSES = 16
TAPS = 49
FH_DEV = 8
MB = 2
NH = 64
NW = 1024
CELLS = 131072
N_ROW = 8


def draw_features(key, part):
    subkeys = jax.random.split(key, 3)
    channel_scale = jnp.exp(jax.random.uniform(subkeys[0], (1, C, 1, 1), jnp.float32, math.log(0.3), math.log(3.0)))
    cell_scale = jnp.exp(jax.random.uniform(subkeys[1], (MB, 1, NH, NW), jnp.float32, math.log(0.3), math.log(3.0)))
    values = jnp.clip(jax.random.normal(subkeys[2], (MB, C, NH, NW), jnp.float32), -4.0, 4.0)
    return (values * channel_scale * cell_scale).astype(jnp.bfloat16)


def draw_w_class(key, part):
    subkeys = jax.random.split(key, 1)
    values = jnp.clip(jax.random.normal(subkeys[0], (LAT, CLASSES), jnp.float32), -4.0, 4.0) * LAT ** (-0.5)
    return values.astype(jnp.bfloat16)


def with_ends(array, own_key, least, largest):
    index_at = [jax.random.randint(jax.random.fold_in(own_key, axis), (), 0, length) for axis, length in enumerate(array.shape)]
    widest = array.shape.index(max(array.shape))
    neighbour = index_at[:widest] + [(index_at[widest] + 1) % array.shape[widest]] + index_at[widest + 1:]
    return array.at[tuple(index_at)].set(least).at[tuple(neighbour)].set(largest)


def centred(own_key, dims, scale, limit, kind=jnp.bfloat16):
    values = jax.random.normal(own_key, dims, jnp.float32) * scale
    return jnp.minimum(jnp.maximum(values, -limit), limit).astype(kind)


def setup_inputs(seed: int = 0) -> dict:
    key_of = jax.random.split(jax.random.key(seed), 16)
    features = draw_features(jax.random.fold_in(key_of[15], 71), 0)
    labels = with_ends(jax.random.randint(key_of[1], (MB, NH, NW), 0, CLASSES), jax.random.fold_in(key_of[1], 1), 0, CLASSES - 1).astype(jnp.int32)
    dw_weight = centred(key_of[2], (C, TAPS), TAPS ** -0.5, 0.875, jnp.float32)
    dw_bias = centred(key_of[3], (C,), 0.5, 3.0, jnp.float32)
    norm_gain = jnp.clip(1.0 + 0.15 * jax.random.normal(key_of[4], (C,), jnp.float32), 0.25, 1.75)
    norm_bias = centred(key_of[5], (C,), 0.3, 2.0, jnp.float32)
    w_in = centred(key_of[6], (C, HID), C ** -0.5, 0.4375)
    b_in = centred(key_of[7], (HID,), 0.5, 3.0, jnp.float32)
    w_out = centred(key_of[8], (HID, C), HID ** -0.5, 0.21875)
    b_out = centred(key_of[9], (C,), 0.5, 3.0, jnp.float32)
    layer_scale = jnp.clip(jnp.exp(jax.random.uniform(key_of[10], (C,), jnp.float32, math.log(0.2), math.log(1.0))), 0.2, 1.0)
    w_lateral = centred(key_of[11], (C, LAT), C ** -0.5, 0.4375)
    b_lateral = centred(key_of[12], (LAT,), 0.5, 3.0, jnp.float32)
    w_class = draw_w_class(jax.random.fold_in(key_of[15], 71), 0)
    b_class = centred(key_of[14], (CLASSES,), 1.0, 4.0, jnp.float32)
    return {"features": features, "labels": labels, "dw_weight": dw_weight, "dw_bias": dw_bias, "norm_gain": norm_gain, "norm_bias": norm_bias, "w_in": w_in, "b_in": b_in, "w_out": w_out, "b_out": b_out, "layer_scale": layer_scale, "w_lateral": w_lateral, "b_lateral": b_lateral, "w_class": w_class, "b_class": b_class}


EPSILON = 1e-06
ROOT_HALF = 0.7071067811865476
DENSITY_SCALE = 0.3989422804014327

def product(form, left_side, right_side):
    return jnp.einsum(form, left_side.astype(jnp.float32), right_side.astype(jnp.float32))

def depthwise(padded, kernel, height, width, flipped):
    total = jnp.zeros((padded.shape[0], height, width), jnp.float32)
    for tap_index in range(49):
        down_step = tap_index // 7
        side_step = tap_index % 7
        if flipped:
            down_step = 6 - down_step
            side_step = 6 - side_step
        window = padded[:, down_step:down_step + height, side_step:side_step + width].astype(jnp.float32)
        total = total + kernel[:, tap_index][:, None, None] * window
    return total

def normal_cdf(values):
    return 0.5 * (1.0 + lax.erf(values * ROOT_HALF))

def gelu_slope(values):
    return normal_cdf(values) + values * jnp.exp(-0.5 * values * values) * DENSITY_SCALE

def encoder_forward(padded, enc_params):
    dw_weight, dw_bias, norm_gain, norm_bias, w_in, b_in, w_out, b_out, layer_scale = enc_params
    height = padded.shape[1] - 6
    width = padded.shape[2] - 6
    conv = depthwise(padded, dw_weight, height, width, False) + dw_bias[:, None, None]
    centre = conv - lax.optimization_barrier(jnp.mean(conv, axis=0, keepdims=True))
    inv_std = lax.rsqrt(lax.optimization_barrier(jnp.mean(centre * centre, axis=0, keepdims=True)) + EPSILON)
    scaled = centre * inv_std
    normed = (scaled * norm_gain[:, None, None] + norm_bias[:, None, None]).astype(jnp.bfloat16)
    before = product('chw,cd->dhw', normed, w_in) + b_in[:, None, None]
    active = (before * normal_cdf(before)).astype(jnp.bfloat16)
    branch = product('dhw,dc->chw', active, w_out) + b_out[:, None, None]
    inner = padded[:, 3:3 + height, 3:3 + width].astype(jnp.float32)
    output = (inner + layer_scale[:, None, None] * branch).astype(jnp.bfloat16)
    return (output, (scaled, inv_std, normed, before, active, branch))

def encoder_backward(saved, grad_out, enc_params):
    dw_weight, dw_bias, norm_gain, norm_bias, w_in, b_in, w_out, b_out, layer_scale = enc_params
    scaled, inv_std, normed, before, active, branch = saved
    grad_float = grad_out.astype(jnp.float32)
    layerscale_grad = lax.optimization_barrier(jnp.sum(branch * grad_float, axis=(1, 2)))
    d_branch = (layer_scale[:, None, None] * grad_float).astype(jnp.bfloat16)
    projbias_grad = lax.optimization_barrier(jnp.sum(d_branch.astype(jnp.float32), axis=(1, 2)))
    project_grad = product('dhw,chw->dc', active, d_branch)
    d_active = product('chw,dc->dhw', d_branch, w_out)
    d_before = (d_active * gelu_slope(before)).astype(jnp.bfloat16)
    expbias_grad = lax.optimization_barrier(jnp.sum(d_before.astype(jnp.float32), axis=(1, 2)))
    expand_grad = product('chw,dhw->cd', normed, d_before)
    d_normed = product('dhw,cd->chw', d_before, w_in)
    gain_grad = lax.optimization_barrier(jnp.sum(d_normed * scaled, axis=(1, 2)))
    normbias_grad = lax.optimization_barrier(jnp.sum(d_normed, axis=(1, 2)))
    d_scaled = d_normed * norm_gain[:, None, None]
    d_conv = inv_std * (d_scaled - lax.optimization_barrier(jnp.mean(d_scaled, axis=0, keepdims=True)) - scaled * lax.optimization_barrier(jnp.mean(d_scaled * scaled, axis=0, keepdims=True)))
    grads = (gain_grad, normbias_grad, expand_grad, expbias_grad, project_grad, projbias_grad, layerscale_grad)
    return (d_conv.astype(jnp.bfloat16), grads)

def conv_backward(padded, d_conv, d_padded, grad_out, dw_weight):
    height = d_conv.shape[1]
    width = d_conv.shape[2]
    d_input = grad_out.astype(jnp.float32) + depthwise(d_padded, dw_weight, height, width, True)
    conv_float = d_conv.astype(jnp.float32)
    columns = []
    for tap_index in range(49):
        down_step = tap_index // 7
        side_step = tap_index % 7
        window = padded[:, down_step:down_step + height, side_step:side_step + width].astype(jnp.float32)
        columns.append(lax.optimization_barrier(jnp.sum(window * conv_float, axis=(1, 2))))
    kernel_grad = jnp.stack(columns, axis=1)
    convbias_grad = lax.optimization_barrier(jnp.sum(conv_float, axis=(1, 2)))
    return (d_input, kernel_grad, convbias_grad)

def decoder(encoded, label_tile, w_lateral, b_lateral, w_class, b_class):
    lateral_pre = product('chw,cl->lhw', encoded, w_lateral) + b_lateral[:, None, None]
    lateral = (lateral_pre * normal_cdf(lateral_pre)).astype(jnp.bfloat16)
    logits = product('lhw,lk->khw', lateral, w_class) + b_class[:, None, None]
    highest = lax.optimization_barrier(jnp.max(logits, axis=0, keepdims=True))
    shifted = logits - highest
    totals = lax.optimization_barrier(jnp.sum(jnp.exp(shifted), axis=0, keepdims=True))
    log_total = highest + jnp.log(totals)
    classes = jnp.arange(logits.shape[0], dtype=jnp.int32)
    onehot = (label_tile[None, :, :] == classes[:, None, None]).astype(jnp.float32)
    loss_sum = jnp.sum(log_total[0] - lax.optimization_barrier(jnp.sum(onehot * logits, axis=0)))
    d_logits = (jnp.exp(shifted) / totals - onehot).astype(jnp.bfloat16)
    classify_grad = product('lhw,khw->lk', lateral, d_logits)
    clsbias_grad = lax.optimization_barrier(jnp.sum(d_logits.astype(jnp.float32), axis=(1, 2)))
    d_lateral_raw = product('khw,lk->lhw', d_logits, w_class)
    d_lateral = (d_lateral_raw * gelu_slope(lateral_pre)).astype(jnp.bfloat16)
    lateral_grad = product('chw,lhw->cl', encoded, d_lateral)
    latbias_grad = lax.optimization_barrier(jnp.sum(d_lateral.astype(jnp.float32), axis=(1, 2)))
    d_encoded = product('lhw,cl->chw', d_lateral, w_lateral).astype(jnp.bfloat16)
    return (d_encoded, loss_sum, (lateral_grad, latbias_grad, classify_grad, clsbias_grad))

def reference(features, labels, dw_weight, dw_bias, norm_gain, norm_bias, w_in, b_in, w_out, b_out, layer_scale, w_lateral, b_lateral, w_class, b_class):
    enc_params = (dw_weight, dw_bias, norm_gain, norm_bias, w_in, b_in, w_out, b_out, layer_scale)
    block_ids = jnp.arange(N_ROW, dtype=jnp.int32)
    totals = None
    inputs_grad = []
    for micro_index in range(MB):
        padded = jnp.pad(features[micro_index], ((0, 0), (3, 3), (3, 3)))
        label_frame = labels[micro_index]

        def first_pass(block_index):
            top_row = (block_index * FH_DEV).astype(jnp.int32)
            anchor = (block_index * 0).astype(jnp.int32)
            block = lax.dynamic_slice(padded, (anchor, top_row, anchor), (C, FH_DEV + 6, NW + 6))
            label_block = lax.dynamic_slice(label_frame, (top_row, anchor), (FH_DEV, NW))
            output, saved = encoder_forward(block, enc_params)
            returned, loss_sum, dec_grads = decoder(output, label_block, w_lateral, b_lateral, w_class, b_class)
            d_conv, enc_grads = encoder_backward(saved, returned, enc_params)
            return (returned, d_conv, loss_sum, dec_grads, enc_grads)
        returned, d_conv, loss_sum, dec_grads, enc_grads = lax.map(first_pass, block_ids)
        returned_whole = jnp.moveaxis(returned, 0, 1).reshape(C, NH, NW)
        conv_whole = jnp.moveaxis(d_conv, 0, 1).reshape(C, NH, NW)
        d_padded = jnp.pad(conv_whole, ((0, 0), (3, 3), (3, 3)))

        def second_pass(block_index):
            top_row = (block_index * FH_DEV).astype(jnp.int32)
            anchor = (block_index * 0).astype(jnp.int32)
            block = lax.dynamic_slice(padded, (anchor, top_row, anchor), (C, FH_DEV + 6, NW + 6))
            grad_block = lax.dynamic_slice(d_padded, (anchor, top_row, anchor), (C, FH_DEV + 6, NW + 6))
            conv_block = lax.dynamic_slice(conv_whole, (anchor, top_row, anchor), (C, FH_DEV, NW))
            return_block = lax.dynamic_slice(returned_whole, (anchor, top_row, anchor), (C, FH_DEV, NW))
            return conv_backward(block, conv_block, grad_block, return_block, dw_weight)
        d_input, kernel_grad, convbias_grad = lax.map(second_pass, block_ids)
        inputs_grad.append(jnp.moveaxis(d_input, 0, 1).reshape(C, NH, NW))
        terms = (lax.optimization_barrier(jnp.sum(kernel_grad, axis=0)), lax.optimization_barrier(jnp.sum(convbias_grad, axis=0))) + tuple((lax.optimization_barrier(jnp.sum(member, axis=0)) for member in enc_grads)) + tuple((lax.optimization_barrier(jnp.sum(member, axis=0)) for member in dec_grads)) + (jnp.sum(loss_sum),)
        totals = terms if totals is None else tuple((left + right for left, right in zip(totals, terms)))
    grad_scale = 1.0 / math.sqrt(CELLS)
    return (jnp.stack(inputs_grad, axis=0), totals[13] / CELLS, totals[0] * grad_scale, totals[1] * grad_scale, totals[2] * grad_scale, totals[3] * grad_scale, totals[4] * grad_scale, totals[5] * grad_scale, totals[6] * grad_scale, totals[7] * grad_scale, totals[8] * grad_scale, totals[9] * grad_scale, totals[10] * grad_scale, totals[11] * grad_scale, totals[12] * grad_scale)
```

```python
import math

import jax
import jax.numpy as jnp
from jax import lax
from jax.sharding import PartitionSpec as P

EPSILON = 1e-06
ROOT_HALF = 0.7071067811865476
DENSITY_SCALE = 0.3989422804014327


def padded_2(x, sides, width):
    for axis, dim in sides:
        count, length = (lax.axis_size(axis), x.shape[dim])
        up = [(i, (i + 1) % count) for i in range(count - 1)]
        down = [(j, i) for i, j in up]
        last = lax.slice_in_dim(x, length - width, length, axis=dim)
        leading = lax.slice_in_dim(x, 0, width, axis=dim)
        before = lax.ppermute(last, axis, up)
        after = lax.ppermute(leading, axis, down)
        x = jnp.concatenate([before, x, after], axis=dim)
    return x


def from_behind(block, axis, distance):
    devices = range(lax.axis_size(axis))
    route = [(i - distance, i) for i in devices if i - distance in devices]
    return lax.ppermute(block, axis, route)


def product(form, left_side, right_side):
    return jnp.einsum(form, left_side, right_side, preferred_element_type=jnp.float32)


def depthwise(padded, kernel, height, width, flipped):
    total = jnp.zeros((padded.shape[0], height, width), jnp.float32)
    for tap_index in range(49):
        down_step = tap_index // 7
        side_step = tap_index % 7
        if flipped:
            down_step = 6 - down_step
            side_step = 6 - side_step
        window = padded[:, down_step : down_step + height, side_step : side_step + width].astype(
            jnp.float32
        )
        total = total + kernel[:, tap_index][:, None, None] * window
    return total


def normal_cdf(values):
    return 0.5 * (1.0 + lax.erf(values * ROOT_HALF))


def gelu_slope(values):
    return normal_cdf(values) + values * jnp.exp(-0.5 * values * values) * DENSITY_SCALE


def encoder_forward(padded, enc_params):
    dw_weight, dw_bias, norm_gain, norm_bias, w_in, b_in, w_out, b_out, layer_scale = enc_params
    height = padded.shape[1] - 6
    width = padded.shape[2] - 6
    conv = depthwise(padded, dw_weight, height, width, False) + dw_bias[:, None, None]
    centre = conv - jnp.mean(conv, axis=0, keepdims=True)
    inv_std = lax.rsqrt(jnp.mean(centre * centre, axis=0, keepdims=True) + EPSILON)
    scaled = centre * inv_std
    normed = (scaled * norm_gain[:, None, None] + norm_bias[:, None, None]).astype(jnp.bfloat16)
    before = product("chw,cd->dhw", normed, w_in) + b_in[:, None, None]
    active = (before * normal_cdf(before)).astype(jnp.bfloat16)
    branch = product("dhw,dc->chw", active, w_out) + b_out[:, None, None]
    inner = padded[:, 3 : 3 + height, 3 : 3 + width].astype(jnp.float32)
    output = (inner + layer_scale[:, None, None] * branch).astype(jnp.bfloat16)
    return (output, (scaled, inv_std, normed, before, active, branch))


def encoder_backward(saved, grad_out, enc_params):
    dw_weight, dw_bias, norm_gain, norm_bias, w_in, b_in, w_out, b_out, layer_scale = enc_params
    scaled, inv_std, normed, before, active, branch = saved
    grad_float = grad_out.astype(jnp.float32)
    layerscale_grad = jnp.sum(branch * grad_float, axis=(1, 2))
    d_branch = (layer_scale[:, None, None] * grad_float).astype(jnp.bfloat16)
    projbias_grad = jnp.sum(d_branch.astype(jnp.float32), axis=(1, 2))
    project_grad = product("dhw,chw->dc", active, d_branch)
    d_active = product("chw,dc->dhw", d_branch, w_out)
    d_before = (d_active * gelu_slope(before)).astype(jnp.bfloat16)
    expbias_grad = jnp.sum(d_before.astype(jnp.float32), axis=(1, 2))
    expand_grad = product("chw,dhw->cd", normed, d_before)
    d_normed = product("dhw,cd->chw", d_before, w_in)
    gain_grad = jnp.sum(d_normed * scaled, axis=(1, 2))
    normbias_grad = jnp.sum(d_normed, axis=(1, 2))
    d_scaled = d_normed * norm_gain[:, None, None]
    d_conv = inv_std * (
        d_scaled
        - jnp.mean(d_scaled, axis=0, keepdims=True)
        - scaled * jnp.mean(d_scaled * scaled, axis=0, keepdims=True)
    )
    grads = (
        gain_grad,
        normbias_grad,
        expand_grad,
        expbias_grad,
        project_grad,
        projbias_grad,
        layerscale_grad,
    )
    return (d_conv.astype(jnp.bfloat16), grads)


def conv_backward(padded, d_conv, d_padded, grad_out, dw_weight):
    height = d_conv.shape[1]
    width = d_conv.shape[2]
    d_input = grad_out.astype(jnp.float32) + depthwise(d_padded, dw_weight, height, width, True)
    conv_float = d_conv.astype(jnp.float32)
    columns = []
    for tap_index in range(49):
        down_step = tap_index // 7
        side_step = tap_index % 7
        window = padded[:, down_step : down_step + height, side_step : side_step + width].astype(
            jnp.float32
        )
        columns.append(jnp.sum(window * conv_float, axis=(1, 2)))
    kernel_grad = jnp.stack(columns, axis=1)
    convbias_grad = jnp.sum(conv_float, axis=(1, 2))
    return (d_input, kernel_grad, convbias_grad)


def decoder(encoded, label_tile, w_lateral, b_lateral, w_class, b_class):
    lateral_pre = product("chw,cl->lhw", encoded, w_lateral) + b_lateral[:, None, None]
    lateral = (lateral_pre * normal_cdf(lateral_pre)).astype(jnp.bfloat16)
    logits = product("lhw,lk->khw", lateral, w_class) + b_class[:, None, None]
    highest = jnp.max(logits, axis=0, keepdims=True)
    shifted = logits - highest
    totals = jnp.sum(jnp.exp(shifted), axis=0, keepdims=True)
    log_total = highest + jnp.log(totals)
    classes = jnp.arange(logits.shape[0], dtype=jnp.int32)
    onehot = (label_tile[None, :, :] == classes[:, None, None]).astype(jnp.float32)
    loss_sum = jnp.sum(log_total[0] - jnp.sum(onehot * logits, axis=0))
    d_logits = (jnp.exp(shifted) / totals - onehot).astype(jnp.bfloat16)
    classify_grad = product("lhw,khw->lk", lateral, d_logits)
    clsbias_grad = jnp.sum(d_logits.astype(jnp.float32), axis=(1, 2))
    d_lateral_raw = product("khw,lk->lhw", d_logits, w_class)
    d_lateral = (d_lateral_raw * gelu_slope(lateral_pre)).astype(jnp.bfloat16)
    lateral_grad = product("chw,lhw->cl", encoded, d_lateral)
    latbias_grad = jnp.sum(d_lateral.astype(jnp.float32), axis=(1, 2))
    d_encoded = product("lhw,cl->chw", d_lateral, w_lateral).astype(jnp.bfloat16)
    return (d_encoded, loss_sum, (lateral_grad, latbias_grad, classify_grad, clsbias_grad))


def flat_psum(parts, axes):
    shapes = [p.shape for p in parts]
    flat = jnp.concatenate([p.reshape(-1) for p in parts])
    total = lax.psum(flat, axes)
    out, at = [], 0
    for shape in shapes:
        size = math.prod(shape)
        out.append(total[at : at + size].reshape(shape))
        at += size
    return out


def shards(
    features,
    labels,
    dw_weight,
    dw_bias,
    norm_gain,
    norm_bias,
    w_in,
    b_in,
    w_out,
    b_out,
    layer_scale,
    w_lateral,
    b_lateral,
    w_class,
    b_class,
):
    enc_params = (dw_weight, dw_bias, norm_gain, norm_bias, w_in, b_in, w_out, b_out, layer_scale)
    section = lax.axis_index("section")
    micro_count = features.shape[0]
    height = features.shape[2]
    width = features.shape[3]
    axes = ("section", "row", "col")

    def rimmed(tile):
        return padded_2(tile, (("row", 1), ("col", 2)), 3)

    tile = lax.dynamic_index_in_dim(features, section, 0, keepdims=False)
    label_tile = lax.dynamic_index_in_dim(labels, section, 0, keepdims=False)
    padded = rimmed(tile)
    output, saved = encoder_forward(padded, enc_params)
    returned, loss_sum, dec_grads = decoder(output, label_tile, w_lateral, b_lateral, w_class, b_class)
    d_conv, enc_grads = encoder_backward(saved, returned, enc_params)
    early = flat_psum(list(enc_grads) + list(dec_grads) + [loss_sum], axes)
    (
        gain_grad,
        normbias_grad,
        expand_grad,
        expbias_grad,
        project_grad,
        projbias_grad,
        layerscale_grad,
        lateral_grad,
        latbias_grad,
        classify_grad,
        clsbias_grad,
        loss_total,
    ) = early
    d_padded = rimmed(d_conv)
    d_input, kernel_grad, convbias_grad = conv_backward(padded, d_conv, d_padded, returned, dw_weight)
    kernel_grad, convbias_grad = flat_psum([kernel_grad, convbias_grad], ("col",))
    kernel_grad, convbias_grad = flat_psum([kernel_grad, convbias_grad], ("row",))
    kernel_grad, convbias_grad = flat_psum([kernel_grad, convbias_grad], ("section",))
    cell_count = micro_count * height * width * lax.axis_size("row") * lax.axis_size("col")
    grad_scale = 1.0 / math.sqrt(cell_count)
    return (
        d_input[None],
        loss_total / cell_count,
        kernel_grad * grad_scale,
        convbias_grad * grad_scale,
        gain_grad * grad_scale,
        normbias_grad * grad_scale,
        expand_grad * grad_scale,
        expbias_grad * grad_scale,
        project_grad * grad_scale,
        projbias_grad * grad_scale,
        layerscale_grad * grad_scale,
        lateral_grad * grad_scale,
        latbias_grad * grad_scale,
        classify_grad * grad_scale,
        clsbias_grad * grad_scale,
    )


def solution(mesh):
    placed = (
        P(None, None, "row", "col"),
        P(None, "row", "col"),
        P(),
        P(),
        P(),
        P(),
        P(),
        P(),
        P(),
        P(),
        P(),
        P(),
        P(),
        P(),
        P(),
    )
    return jax.shard_map(
        shards,
        mesh=mesh,
        in_specs=placed,
        out_specs=(
            P("section", None, "row", "col"),
            P(),
            P(),
            P(),
            P(),
            P(),
            P(),
            P(),
            P(),
            P(),
            P(),
            P(),
            P(),
            P(),
            P(),
        ),
        check_vma=False,
    )
```

```python
import math

import jax
import jax.numpy as jnp
from jax import lax
from jax.sharding import PartitionSpec as P

EPSILON = 1e-06
ROOT_HALF = 0.7071067811865476
DENSITY_SCALE = 0.3989422804014327


def padded_2(x, sides, width):
    for axis, dim in sides:
        count, length = (lax.axis_size(axis), x.shape[dim])
        up = [(i, (i + 1) % count) for i in range(count - 1)]
        down = [(j, i) for i, j in up]
        last = lax.slice_in_dim(x, length - width, length, axis=dim)
        leading = lax.slice_in_dim(x, 0, width, axis=dim)
        before = lax.ppermute(last, axis, up)
        after = lax.ppermute(leading, axis, down)
        x = jnp.concatenate([before, x, after], axis=dim)
    return x


def from_behind(block, axis, distance):
    devices = range(lax.axis_size(axis))
    route = [(i - distance, i) for i in devices if i - distance in devices]
    return lax.ppermute(block, axis, route)


def product(form, left_side, right_side):
    return jnp.einsum(form, left_side, right_side, preferred_element_type=jnp.float32)


def depthwise(padded, kernel, height, width, flipped):
    total = jnp.zeros((padded.shape[0], height, width), jnp.float32)
    for tap_index in range(49):
        down_step = tap_index // 7
        side_step = tap_index % 7
        if flipped:
            down_step = 6 - down_step
            side_step = 6 - side_step
        window = padded[:, down_step : down_step + height, side_step : side_step + width].astype(
            jnp.float32
        )
        total = total + kernel[:, tap_index][:, None, None] * window
    return total


def normal_cdf(values):
    return 0.5 * (1.0 + lax.erf(values * ROOT_HALF))


def gelu_slope(values):
    return normal_cdf(values) + values * jnp.exp(-0.5 * values * values) * DENSITY_SCALE


def encoder_forward(padded, enc_params):
    dw_weight, dw_bias, norm_gain, norm_bias, w_in, b_in, w_out, b_out, layer_scale = enc_params
    height = padded.shape[1] - 6
    width = padded.shape[2] - 6
    conv = depthwise(padded, dw_weight, height, width, False) + dw_bias[:, None, None]
    centre = conv - jnp.mean(conv, axis=0, keepdims=True)
    inv_std = lax.rsqrt(jnp.mean(centre * centre, axis=0, keepdims=True) + EPSILON)
    scaled = centre * inv_std
    normed = (scaled * norm_gain[:, None, None] + norm_bias[:, None, None]).astype(jnp.bfloat16)
    before = product("chw,cd->dhw", normed, w_in) + b_in[:, None, None]
    active = (before * normal_cdf(before)).astype(jnp.bfloat16)
    branch = product("dhw,dc->chw", active, w_out) + b_out[:, None, None]
    inner = padded[:, 3 : 3 + height, 3 : 3 + width].astype(jnp.float32)
    output = (inner + layer_scale[:, None, None] * branch).astype(jnp.bfloat16)
    return (output, (scaled, inv_std, normed, before, active, branch))


def encoder_backward(saved, grad_out, enc_params):
    dw_weight, dw_bias, norm_gain, norm_bias, w_in, b_in, w_out, b_out, layer_scale = enc_params
    scaled, inv_std, normed, before, active, branch = saved
    grad_float = grad_out.astype(jnp.float32)
    layerscale_grad = jnp.sum(branch * grad_float, axis=(1, 2))
    d_branch = (layer_scale[:, None, None] * grad_float).astype(jnp.bfloat16)
    projbias_grad = jnp.sum(d_branch.astype(jnp.float32), axis=(1, 2))
    project_grad = product("dhw,chw->dc", active, d_branch)
    d_active = product("chw,dc->dhw", d_branch, w_out)
    d_before = (d_active * gelu_slope(before)).astype(jnp.bfloat16)
    expbias_grad = jnp.sum(d_before.astype(jnp.float32), axis=(1, 2))
    expand_grad = product("chw,dhw->cd", normed, d_before)
    d_normed = product("dhw,cd->chw", d_before, w_in)
    gain_grad = jnp.sum(d_normed * scaled, axis=(1, 2))
    normbias_grad = jnp.sum(d_normed, axis=(1, 2))
    d_scaled = d_normed * norm_gain[:, None, None]
    d_conv = inv_std * (
        d_scaled
        - jnp.mean(d_scaled, axis=0, keepdims=True)
        - scaled * jnp.mean(d_scaled * scaled, axis=0, keepdims=True)
    )
    grads = (
        gain_grad,
        normbias_grad,
        expand_grad,
        expbias_grad,
        project_grad,
        projbias_grad,
        layerscale_grad,
    )
    return (d_conv.astype(jnp.bfloat16), grads)


def conv_backward(padded, d_conv, d_padded, grad_out, dw_weight):
    height = d_conv.shape[1]
    width = d_conv.shape[2]
    d_input = grad_out.astype(jnp.float32) + depthwise(d_padded, dw_weight, height, width, True)
    conv_float = d_conv.astype(jnp.float32)
    columns = []
    for tap_index in range(49):
        down_step = tap_index // 7
        side_step = tap_index % 7
        window = padded[:, down_step : down_step + height, side_step : side_step + width].astype(
            jnp.float32
        )
        columns.append(jnp.sum(window * conv_float, axis=(1, 2)))
    kernel_grad = jnp.stack(columns, axis=1)
    convbias_grad = jnp.sum(conv_float, axis=(1, 2))
    return (d_input, kernel_grad, convbias_grad)


def decoder(encoded, label_tile, w_lateral, b_lateral, w_class, b_class):
    lateral_pre = product("chw,cl->lhw", encoded, w_lateral) + b_lateral[:, None, None]
    lateral = (lateral_pre * normal_cdf(lateral_pre)).astype(jnp.bfloat16)
    logits = product("lhw,lk->khw", lateral, w_class) + b_class[:, None, None]
    highest = jnp.max(logits, axis=0, keepdims=True)
    shifted = logits - highest
    totals = jnp.sum(jnp.exp(shifted), axis=0, keepdims=True)
    log_total = highest + jnp.log(totals)
    classes = jnp.arange(logits.shape[0], dtype=jnp.int32)
    onehot = (label_tile[None, :, :] == classes[:, None, None]).astype(jnp.float32)
    loss_sum = jnp.sum(log_total[0] - jnp.sum(onehot * logits, axis=0))
    d_logits = (jnp.exp(shifted) / totals - onehot).astype(jnp.bfloat16)
    classify_grad = product("lhw,khw->lk", lateral, d_logits)
    clsbias_grad = jnp.sum(d_logits.astype(jnp.float32), axis=(1, 2))
    d_lateral_raw = product("khw,lk->lhw", d_logits, w_class)
    d_lateral = (d_lateral_raw * gelu_slope(lateral_pre)).astype(jnp.bfloat16)
    lateral_grad = product("chw,lhw->cl", encoded, d_lateral)
    latbias_grad = jnp.sum(d_lateral.astype(jnp.float32), axis=(1, 2))
    d_encoded = product("lhw,cl->chw", d_lateral, w_lateral).astype(jnp.bfloat16)
    return (d_encoded, loss_sum, (lateral_grad, latbias_grad, classify_grad, clsbias_grad))


LANES = 128


def pack_rows(parts, multiple):
    shapes, rows = [], []
    for part in parts:
        flat = part.reshape(-1)
        size = flat.shape[0]
        padded_rows = -(-size // (8 * LANES)) * 8
        flat = jnp.pad(flat, (0, padded_rows * LANES - size))
        rows.append(flat.reshape(padded_rows, LANES))
        shapes.append(part.shape)
    total = sum(r.shape[0] for r in rows)
    extra = -total % multiple
    if extra:
        rows.append(jnp.zeros((extra, LANES), jnp.float32))
    return jnp.concatenate(rows, axis=0), shapes


def unpack_rows(buffer, shapes):
    out, at = [], 0
    for shape in shapes:
        size = math.prod(shape)
        padded_rows = -(-size // (8 * LANES)) * 8
        out.append(buffer[at : at + padded_rows].reshape(-1)[:size].reshape(shape))
        at += padded_rows
    return out


def butterfly_psum(buffer, axes, order):
    index = lax.axis_index(axes)
    count = math.prod(lax.axis_size(a) for a in axes)
    for bit_at in order:
        bit = (index >> bit_at) & 1
        halves = buffer.reshape(2, buffer.shape[0] // 2, buffer.shape[1])
        keep = lax.dynamic_index_in_dim(halves, bit, 0, keepdims=False)
        send = lax.dynamic_index_in_dim(halves, 1 - bit, 0, keepdims=False)
        pairs = [(i, i ^ (1 << bit_at)) for i in range(count)]
        buffer = keep + lax.ppermute(send, axes, pairs)
    for bit_at in reversed(order):
        bit = (index >> bit_at) & 1
        pairs = [(i, i ^ (1 << bit_at)) for i in range(count)]
        other = lax.ppermute(buffer, axes, pairs)
        both = jnp.zeros((2,) + buffer.shape, buffer.dtype)
        both = lax.dynamic_update_index_in_dim(both, buffer, bit, 0)
        both = lax.dynamic_update_index_in_dim(both, other, 1 - bit, 0)
        buffer = both.reshape(-1, buffer.shape[1])
    return buffer


def shards(
    features,
    labels,
    dw_weight,
    dw_bias,
    norm_gain,
    norm_bias,
    w_in,
    b_in,
    w_out,
    b_out,
    layer_scale,
    w_lateral,
    b_lateral,
    w_class,
    b_class,
):
    enc_params = (dw_weight, dw_bias, norm_gain, norm_bias, w_in, b_in, w_out, b_out, layer_scale)
    section = lax.axis_index("section")
    micro_count = features.shape[0]
    height = features.shape[2]
    width = features.shape[3]
    axes = ("section", "row", "col")

    def rimmed(tile):
        return padded_2(tile, (("row", 1), ("col", 2)), 3)

    tile = lax.dynamic_index_in_dim(features, section, 0, keepdims=False)
    label_tile = lax.dynamic_index_in_dim(labels, section, 0, keepdims=False)
    padded = rimmed(tile)
    output, saved = encoder_forward(padded, enc_params)
    returned, loss_sum, dec_grads = decoder(output, label_tile, w_lateral, b_lateral, w_class, b_class)
    d_conv, enc_grads = encoder_backward(saved, returned, enc_params)
    d_padded = rimmed(d_conv)
    d_input, kernel_grad, convbias_grad = conv_backward(padded, d_conv, d_padded, returned, dw_weight)
    parts = [kernel_grad, convbias_grad] + list(enc_grads) + list(dec_grads) + [loss_sum]
    count = math.prod(lax.axis_size(a) for a in axes)
    buffer, shapes = pack_rows(parts, count * 2)
    buffer = butterfly_psum(buffer, axes, [3, 6, 1, 2, 0, 4, 5])
    (
        kernel_grad,
        convbias_grad,
        gain_grad,
        normbias_grad,
        expand_grad,
        expbias_grad,
        project_grad,
        projbias_grad,
        layerscale_grad,
        lateral_grad,
        latbias_grad,
        classify_grad,
        clsbias_grad,
        loss_total,
    ) = unpack_rows(buffer, shapes)
    cell_count = micro_count * height * width * lax.axis_size("row") * lax.axis_size("col")
    grad_scale = 1.0 / math.sqrt(cell_count)
    return (
        d_input[None],
        loss_total / cell_count,
        kernel_grad * grad_scale,
        convbias_grad * grad_scale,
        gain_grad * grad_scale,
        normbias_grad * grad_scale,
        expand_grad * grad_scale,
        expbias_grad * grad_scale,
        project_grad * grad_scale,
        projbias_grad * grad_scale,
        layerscale_grad * grad_scale,
        lateral_grad * grad_scale,
        latbias_grad * grad_scale,
        classify_grad * grad_scale,
        clsbias_grad * grad_scale,
    )


def solution(mesh):
    placed = (
        P(None, None, "row", "col"),
        P(None, "row", "col"),
        P(),
        P(),
        P(),
        P(),
        P(),
        P(),
        P(),
        P(),
        P(),
        P(),
        P(),
        P(),
        P(),
    )
    return jax.shard_map(
        shards,
        mesh=mesh,
        in_specs=placed,
        out_specs=(
            P("section", None, "row", "col"),
            P(),
            P(),
            P(),
            P(),
            P(),
            P(),
            P(),
            P(),
            P(),
            P(),
            P(),
            P(),
            P(),
            P(),
        ),
        check_vma=False,
    )
```

```python
import math

import jax
import jax.numpy as jnp
from jax import lax
from jax.sharding import PartitionSpec as P

EPSILON = 1e-06
ROOT_HALF = 0.7071067811865476
DENSITY_SCALE = 0.3989422804014327


def padded_2(x, sides, width):
    for axis, dim in sides:
        count, length = (lax.axis_size(axis), x.shape[dim])
        up = [(i, (i + 1) % count) for i in range(count - 1)]
        down = [(j, i) for i, j in up]
        last = lax.slice_in_dim(x, length - width, length, axis=dim)
        leading = lax.slice_in_dim(x, 0, width, axis=dim)
        before = lax.ppermute(last, axis, up)
        after = lax.ppermute(leading, axis, down)
        x = jnp.concatenate([before, x, after], axis=dim)
    return x


def from_behind(block, axis, distance):
    devices = range(lax.axis_size(axis))
    route = [(i - distance, i) for i in devices if i - distance in devices]
    return lax.ppermute(block, axis, route)


def product(form, left_side, right_side):
    return jnp.einsum(form, left_side, right_side, preferred_element_type=jnp.float32)


def depthwise(padded, kernel, height, width, flipped):
    total = jnp.zeros((padded.shape[0], height, width), jnp.float32)
    for tap_index in range(49):
        down_step = tap_index // 7
        side_step = tap_index % 7
        if flipped:
            down_step = 6 - down_step
            side_step = 6 - side_step
        window = padded[:, down_step : down_step + height, side_step : side_step + width].astype(
            jnp.float32
        )
        total = total + kernel[:, tap_index][:, None, None] * window
    return total


def normal_cdf(values):
    return 0.5 * (1.0 + lax.erf(values * ROOT_HALF))


def gelu_slope(values):
    return normal_cdf(values) + values * jnp.exp(-0.5 * values * values) * DENSITY_SCALE


def encoder_forward(padded, enc_params):
    dw_weight, dw_bias, norm_gain, norm_bias, w_in, b_in, w_out, b_out, layer_scale = enc_params
    height = padded.shape[1] - 6
    width = padded.shape[2] - 6
    conv = depthwise(padded, dw_weight, height, width, False) + dw_bias[:, None, None]
    centre = conv - jnp.mean(conv, axis=0, keepdims=True)
    inv_std = lax.rsqrt(jnp.mean(centre * centre, axis=0, keepdims=True) + EPSILON)
    scaled = centre * inv_std
    normed = (scaled * norm_gain[:, None, None] + norm_bias[:, None, None]).astype(jnp.bfloat16)
    before = product("chw,cd->dhw", normed, w_in) + b_in[:, None, None]
    active = (before * normal_cdf(before)).astype(jnp.bfloat16)
    branch = product("dhw,dc->chw", active, w_out) + b_out[:, None, None]
    inner = padded[:, 3 : 3 + height, 3 : 3 + width].astype(jnp.float32)
    output = (inner + layer_scale[:, None, None] * branch).astype(jnp.bfloat16)
    return (output, (scaled, inv_std, normed, before, active, branch))


def encoder_backward(saved, grad_out, enc_params):
    dw_weight, dw_bias, norm_gain, norm_bias, w_in, b_in, w_out, b_out, layer_scale = enc_params
    scaled, inv_std, normed, before, active, branch = saved
    grad_float = grad_out.astype(jnp.float32)
    layerscale_grad = jnp.sum(branch * grad_float, axis=(1, 2))
    d_branch = (layer_scale[:, None, None] * grad_float).astype(jnp.bfloat16)
    projbias_grad = jnp.sum(d_branch.astype(jnp.float32), axis=(1, 2))
    project_grad = product("dhw,chw->dc", active, d_branch)
    d_active = product("chw,dc->dhw", d_branch, w_out)
    d_before = (d_active * gelu_slope(before)).astype(jnp.bfloat16)
    expbias_grad = jnp.sum(d_before.astype(jnp.float32), axis=(1, 2))
    expand_grad = product("chw,dhw->cd", normed, d_before)
    d_normed = product("dhw,cd->chw", d_before, w_in)
    gain_grad = jnp.sum(d_normed * scaled, axis=(1, 2))
    normbias_grad = jnp.sum(d_normed, axis=(1, 2))
    d_scaled = d_normed * norm_gain[:, None, None]
    d_conv = inv_std * (
        d_scaled
        - jnp.mean(d_scaled, axis=0, keepdims=True)
        - scaled * jnp.mean(d_scaled * scaled, axis=0, keepdims=True)
    )
    grads = (
        gain_grad,
        normbias_grad,
        expand_grad,
        expbias_grad,
        project_grad,
        projbias_grad,
        layerscale_grad,
    )
    return (d_conv.astype(jnp.bfloat16), grads)


def conv_backward(padded, d_conv, d_padded, grad_out, dw_weight):
    height = d_conv.shape[1]
    width = d_conv.shape[2]
    d_input = grad_out.astype(jnp.float32) + depthwise(d_padded, dw_weight, height, width, True)
    conv_float = d_conv.astype(jnp.float32)
    columns = []
    for tap_index in range(49):
        down_step = tap_index // 7
        side_step = tap_index % 7
        window = padded[:, down_step : down_step + height, side_step : side_step + width].astype(
            jnp.float32
        )
        columns.append(jnp.sum(window * conv_float, axis=(1, 2)))
    kernel_grad = jnp.stack(columns, axis=1)
    convbias_grad = jnp.sum(conv_float, axis=(1, 2))
    return (d_input, kernel_grad, convbias_grad)


def decoder(encoded, label_tile, w_lateral, b_lateral, w_class, b_class):
    lateral_pre = product("chw,cl->lhw", encoded, w_lateral) + b_lateral[:, None, None]
    lateral = (lateral_pre * normal_cdf(lateral_pre)).astype(jnp.bfloat16)
    logits = product("lhw,lk->khw", lateral, w_class) + b_class[:, None, None]
    highest = jnp.max(logits, axis=0, keepdims=True)
    shifted = logits - highest
    totals = jnp.sum(jnp.exp(shifted), axis=0, keepdims=True)
    log_total = highest + jnp.log(totals)
    classes = jnp.arange(logits.shape[0], dtype=jnp.int32)
    onehot = (label_tile[None, :, :] == classes[:, None, None]).astype(jnp.float32)
    loss_sum = jnp.sum(log_total[0] - jnp.sum(onehot * logits, axis=0))
    d_logits = (jnp.exp(shifted) / totals - onehot).astype(jnp.bfloat16)
    classify_grad = product("lhw,khw->lk", lateral, d_logits)
    clsbias_grad = jnp.sum(d_logits.astype(jnp.float32), axis=(1, 2))
    d_lateral_raw = product("khw,lk->lhw", d_logits, w_class)
    d_lateral = (d_lateral_raw * gelu_slope(lateral_pre)).astype(jnp.bfloat16)
    lateral_grad = product("chw,lhw->cl", encoded, d_lateral)
    latbias_grad = jnp.sum(d_lateral.astype(jnp.float32), axis=(1, 2))
    d_encoded = product("lhw,cl->chw", d_lateral, w_lateral).astype(jnp.bfloat16)
    return (d_encoded, loss_sum, (lateral_grad, latbias_grad, classify_grad, clsbias_grad))


LANES = 128


def pack_rows(parts, multiple):
    shapes, rows = [], []
    for part in parts:
        flat = part.reshape(-1)
        size = flat.shape[0]
        padded_rows = -(-size // (8 * LANES)) * 8
        flat = jnp.pad(flat, (0, padded_rows * LANES - size))
        rows.append(flat.reshape(padded_rows, LANES))
        shapes.append(part.shape)
    total = sum(r.shape[0] for r in rows)
    extra = -total % multiple
    if extra:
        rows.append(jnp.zeros((extra, LANES), jnp.float32))
    return jnp.concatenate(rows, axis=0), shapes


def unpack_rows(buffer, shapes):
    out, at = [], 0
    for shape in shapes:
        size = math.prod(shape)
        padded_rows = -(-size // (8 * LANES)) * 8
        out.append(buffer[at : at + padded_rows].reshape(-1)[:size].reshape(shape))
        at += padded_rows
    return out


def spread(value, bits):
    out = 0
    for k, bit_at in enumerate(bits):
        if (value >> k) & 1:
            out |= 1 << bit_at
    return out


def butterfly_psum(buffer, axes, stages, scale_of):
    index = lax.axis_index(axes)
    count = math.prod(lax.axis_size(a) for a in axes)
    offset = jnp.zeros((), jnp.int32)
    places = []
    for bits in stages:
        ways = 1 << len(bits)
        mine = sum(((index >> bit_at) & 1) << k for k, bit_at in enumerate(bits))
        pieces = buffer.reshape(ways, buffer.shape[0] // ways, buffer.shape[1])
        total = lax.dynamic_index_in_dim(pieces, mine, 0, keepdims=False)
        for step in range(1, ways):
            flip = spread(step, bits)
            pairs = [(i, i ^ flip) for i in range(count)]
            send = lax.dynamic_index_in_dim(pieces, mine ^ step, 0, keepdims=False)
            total = total + lax.ppermute(send, axes, pairs)
        offset = offset * ways + mine
        places.append((bits, mine))
        buffer = total
    rows = buffer.shape[0]
    position = (offset * rows + lax.broadcasted_iota(jnp.int32, buffer.shape, 0)) * buffer.shape[1]
    position = position + lax.broadcasted_iota(jnp.int32, buffer.shape, 1)
    buffer = buffer * scale_of(position)
    for bits, mine in reversed(places):
        ways = 1 << len(bits)
        both = jnp.zeros((ways,) + buffer.shape, buffer.dtype)
        both = lax.dynamic_update_index_in_dim(both, buffer, mine, 0)
        for step in range(1, ways):
            flip = spread(step, bits)
            pairs = [(i, i ^ flip) for i in range(count)]
            other = lax.ppermute(buffer, axes, pairs)
            both = lax.dynamic_update_index_in_dim(both, other, mine ^ step, 0)
        buffer = both.reshape(-1, buffer.shape[1])
    return buffer


def shards(
    features,
    labels,
    dw_weight,
    dw_bias,
    norm_gain,
    norm_bias,
    w_in,
    b_in,
    w_out,
    b_out,
    layer_scale,
    w_lateral,
    b_lateral,
    w_class,
    b_class,
):
    enc_params = (dw_weight, dw_bias, norm_gain, norm_bias, w_in, b_in, w_out, b_out, layer_scale)
    section = lax.axis_index("section")
    micro_count = features.shape[0]
    height = features.shape[2]
    width = features.shape[3]
    axes = ("section", "row", "col")

    def rimmed(tile):
        return padded_2(tile, (("row", 1), ("col", 2)), 3)

    tile = lax.dynamic_index_in_dim(features, section, 0, keepdims=False)
    label_tile = lax.dynamic_index_in_dim(labels, section, 0, keepdims=False)
    padded = rimmed(tile)
    output, saved = encoder_forward(padded, enc_params)
    returned, loss_sum, dec_grads = decoder(output, label_tile, w_lateral, b_lateral, w_class, b_class)
    d_conv, enc_grads = encoder_backward(saved, returned, enc_params)
    d_padded = rimmed(d_conv)
    d_input, kernel_grad, convbias_grad = conv_backward(padded, d_conv, d_padded, returned, dw_weight)
    (
        gain_grad,
        normbias_grad,
        expand_grad,
        expbias_grad,
        project_grad,
        projbias_grad,
        layerscale_grad,
    ) = enc_grads
    lateral_grad, latbias_grad, classify_grad, clsbias_grad = dec_grads
    vectors = [convbias_grad, gain_grad, normbias_grad, expbias_grad, projbias_grad]
    vectors += [layerscale_grad, latbias_grad, clsbias_grad, loss_sum.reshape(1)]
    joined = jnp.concatenate(vectors)
    parts = [joined, kernel_grad, expand_grad, project_grad, lateral_grad, classify_grad]
    count = math.prod(lax.axis_size(a) for a in axes)
    buffer, shapes = pack_rows(parts, count * 2)
    buffer, d_padded = lax.optimization_barrier((buffer, d_padded))
    d_input, _, _ = conv_backward(padded, d_conv, d_padded, returned, dw_weight)
    cell_count = micro_count * height * width * lax.axis_size("row") * lax.axis_size("col")
    grad_scale = 1.0 / math.sqrt(cell_count)
    loss_at = joined.shape[0] - 1

    def scale_of(position):
        return jnp.where(position == loss_at, 1.0 / cell_count, grad_scale).astype(jnp.float32)

    buffer = butterfly_psum(buffer, axes, [(3,), (6, 0), (1, 2), (4, 5)], scale_of)
    joined, kernel_grad, expand_grad, project_grad, lateral_grad, classify_grad = unpack_rows(
        buffer, shapes
    )
    sizes = [v.shape[0] for v in vectors]
    cuts = [sum(sizes[:k]) for k in range(len(sizes) + 1)]
    (
        convbias_grad,
        gain_grad,
        normbias_grad,
        expbias_grad,
        projbias_grad,
        layerscale_grad,
        latbias_grad,
        clsbias_grad,
        loss_total,
    ) = [joined[cuts[k] : cuts[k + 1]] for k in range(len(sizes))]
    return (
        d_input[None],
        loss_total[0],
        kernel_grad,
        convbias_grad,
        gain_grad,
        normbias_grad,
        expand_grad,
        expbias_grad,
        project_grad,
        projbias_grad,
        layerscale_grad,
        lateral_grad,
        latbias_grad,
        classify_grad,
        clsbias_grad,
    )


def solution(mesh):
    placed = (
        P(None, None, "row", "col"),
        P(None, "row", "col"),
        P(),
        P(),
        P(),
        P(),
        P(),
        P(),
        P(),
        P(),
        P(),
        P(),
        P(),
        P(),
        P(),
    )
    return jax.shard_map(
        shards,
        mesh=mesh,
        in_specs=placed,
        out_specs=(
            P("section", None, "row", "col"),
            P(),
            P(),
            P(),
            P(),
            P(),
            P(),
            P(),
            P(),
            P(),
            P(),
            P(),
            P(),
            P(),
            P(),
        ),
        check_vma=False,
    )
```

```python
import math

import jax
import jax.numpy as jnp
from jax import lax
from jax.sharding import PartitionSpec as P

EPSILON = 1e-06
ROOT_HALF = 0.7071067811865476
DENSITY_SCALE = 0.3989422804014327


def padded_2(x, sides, width):
    for axis, dim in sides:
        count, length = (lax.axis_size(axis), x.shape[dim])
        up = [(i, (i + 1) % count) for i in range(count - 1)]
        down = [(j, i) for i, j in up]
        last = lax.slice_in_dim(x, length - width, length, axis=dim)
        leading = lax.slice_in_dim(x, 0, width, axis=dim)
        before = lax.ppermute(last, axis, up)
        after = lax.ppermute(leading, axis, down)
        x = jnp.concatenate([before, x, after], axis=dim)
    return x


def from_behind(block, axis, distance):
    devices = range(lax.axis_size(axis))
    route = [(i - distance, i) for i in devices if i - distance in devices]
    return lax.ppermute(block, axis, route)


def product(form, left_side, right_side):
    return jnp.einsum(form, left_side, right_side, preferred_element_type=jnp.float32)


def depthwise(padded, kernel, height, width, flipped):
    total = jnp.zeros((padded.shape[0], height, width), jnp.float32)
    for tap_index in range(49):
        down_step = tap_index // 7
        side_step = tap_index % 7
        if flipped:
            down_step = 6 - down_step
            side_step = 6 - side_step
        window = padded[:, down_step : down_step + height, side_step : side_step + width].astype(
            jnp.float32
        )
        total = total + kernel[:, tap_index][:, None, None] * window
    return total


def normal_cdf(values):
    return 0.5 * (1.0 + lax.erf(values * ROOT_HALF))


def gelu_slope(values):
    return normal_cdf(values) + values * jnp.exp(-0.5 * values * values) * DENSITY_SCALE


def encoder_forward(padded, enc_params):
    dw_weight, dw_bias, norm_gain, norm_bias, w_in, b_in, w_out, b_out, layer_scale = enc_params
    height = padded.shape[1] - 6
    width = padded.shape[2] - 6
    conv = depthwise(padded, dw_weight, height, width, False) + dw_bias[:, None, None]
    centre = conv - jnp.mean(conv, axis=0, keepdims=True)
    inv_std = lax.rsqrt(jnp.mean(centre * centre, axis=0, keepdims=True) + EPSILON)
    scaled = centre * inv_std
    normed = (scaled * norm_gain[:, None, None] + norm_bias[:, None, None]).astype(jnp.bfloat16)
    before = product("chw,cd->dhw", normed, w_in) + b_in[:, None, None]
    active = (before * normal_cdf(before)).astype(jnp.bfloat16)
    branch = product("dhw,dc->chw", active, w_out) + b_out[:, None, None]
    inner = padded[:, 3 : 3 + height, 3 : 3 + width].astype(jnp.float32)
    output = (inner + layer_scale[:, None, None] * branch).astype(jnp.bfloat16)
    return (output, (scaled, inv_std, normed, before, active, branch))


def encoder_backward(saved, grad_out, enc_params):
    dw_weight, dw_bias, norm_gain, norm_bias, w_in, b_in, w_out, b_out, layer_scale = enc_params
    scaled, inv_std, normed, before, active, branch = saved
    grad_float = grad_out.astype(jnp.float32)
    layerscale_grad = jnp.sum(branch * grad_float, axis=(1, 2))
    d_branch = (layer_scale[:, None, None] * grad_float).astype(jnp.bfloat16)
    projbias_grad = jnp.sum(d_branch.astype(jnp.float32), axis=(1, 2))
    project_grad = product("dhw,chw->dc", active, d_branch)
    d_active = product("chw,dc->dhw", d_branch, w_out)
    d_before = (d_active * gelu_slope(before)).astype(jnp.bfloat16)
    expbias_grad = jnp.sum(d_before.astype(jnp.float32), axis=(1, 2))
    expand_grad = product("chw,dhw->cd", normed, d_before)
    d_normed = product("dhw,cd->chw", d_before, w_in)
    gain_grad = jnp.sum(d_normed * scaled, axis=(1, 2))
    normbias_grad = jnp.sum(d_normed, axis=(1, 2))
    d_scaled = d_normed * norm_gain[:, None, None]
    d_conv = inv_std * (
        d_scaled
        - jnp.mean(d_scaled, axis=0, keepdims=True)
        - scaled * jnp.mean(d_scaled * scaled, axis=0, keepdims=True)
    )
    grads = (
        gain_grad,
        normbias_grad,
        expand_grad,
        expbias_grad,
        project_grad,
        projbias_grad,
        layerscale_grad,
    )
    return (d_conv.astype(jnp.bfloat16), grads)


def conv_backward(padded, d_conv, d_padded, grad_out, dw_weight):
    height = d_conv.shape[1]
    width = d_conv.shape[2]
    d_input = grad_out.astype(jnp.float32) + depthwise(d_padded, dw_weight, height, width, True)
    conv_float = d_conv.astype(jnp.float32)
    columns = []
    for tap_index in range(49):
        down_step = tap_index // 7
        side_step = tap_index % 7
        window = padded[:, down_step : down_step + height, side_step : side_step + width].astype(
            jnp.float32
        )
        columns.append(jnp.sum(window * conv_float, axis=(1, 2)))
    kernel_grad = jnp.stack(columns, axis=1)
    convbias_grad = jnp.sum(conv_float, axis=(1, 2))
    return (d_input, kernel_grad, convbias_grad)


def decoder(encoded, label_tile, w_lateral, b_lateral, w_class, b_class):
    lateral_pre = product("chw,cl->lhw", encoded, w_lateral) + b_lateral[:, None, None]
    lateral = (lateral_pre * normal_cdf(lateral_pre)).astype(jnp.bfloat16)
    logits = product("lhw,lk->khw", lateral, w_class) + b_class[:, None, None]
    highest = jnp.max(logits, axis=0, keepdims=True)
    shifted = logits - highest
    totals = jnp.sum(jnp.exp(shifted), axis=0, keepdims=True)
    log_total = highest + jnp.log(totals)
    classes = jnp.arange(logits.shape[0], dtype=jnp.int32)
    onehot = (label_tile[None, :, :] == classes[:, None, None]).astype(jnp.float32)
    loss_sum = jnp.sum(log_total[0] - jnp.sum(onehot * logits, axis=0))
    d_logits = (jnp.exp(shifted) / totals - onehot).astype(jnp.bfloat16)
    classify_grad = product("lhw,khw->lk", lateral, d_logits)
    clsbias_grad = jnp.sum(d_logits.astype(jnp.float32), axis=(1, 2))
    d_lateral_raw = product("khw,lk->lhw", d_logits, w_class)
    d_lateral = (d_lateral_raw * gelu_slope(lateral_pre)).astype(jnp.bfloat16)
    lateral_grad = product("chw,lhw->cl", encoded, d_lateral)
    latbias_grad = jnp.sum(d_lateral.astype(jnp.float32), axis=(1, 2))
    d_encoded = product("lhw,cl->chw", d_lateral, w_lateral).astype(jnp.bfloat16)
    return (d_encoded, loss_sum, (lateral_grad, latbias_grad, classify_grad, clsbias_grad))


LANES = 128


def pack_rows(parts, multiple):
    shapes, rows = [], []
    for part in parts:
        flat = part.reshape(-1)
        size = flat.shape[0]
        padded_rows = -(-size // (8 * LANES)) * 8
        flat = jnp.pad(flat, (0, padded_rows * LANES - size))
        rows.append(flat.reshape(padded_rows, LANES))
        shapes.append(part.shape)
    total = sum(r.shape[0] for r in rows)
    extra = -total % multiple
    if extra:
        rows.append(jnp.zeros((extra, LANES), jnp.float32))
    return jnp.concatenate(rows, axis=0), shapes


def unpack_rows(buffer, shapes):
    out, at = [], 0
    for shape in shapes:
        size = math.prod(shape)
        padded_rows = -(-size // (8 * LANES)) * 8
        out.append(buffer[at : at + padded_rows].reshape(-1)[:size].reshape(shape))
        at += padded_rows
    return out


def spread(value, bits):
    out = 0
    for k, bit_at in enumerate(bits):
        if (value >> k) & 1:
            out |= 1 << bit_at
    return out


def butterfly_psum(buffer, axes, stages, scale_of, tie, tie_after):
    index = lax.axis_index(axes)
    count = math.prod(lax.axis_size(a) for a in axes)
    offset = jnp.zeros((), jnp.int32)
    places = []
    for bits in stages:
        ways = 1 << len(bits)
        mine = sum(((index >> bit_at) & 1) << k for k, bit_at in enumerate(bits))
        pieces = buffer.reshape(ways, buffer.shape[0] // ways, buffer.shape[1])
        total = lax.dynamic_index_in_dim(pieces, mine, 0, keepdims=False)
        for step in range(1, ways):
            flip = spread(step, bits)
            pairs = [(i, i ^ flip) for i in range(count)]
            send = lax.dynamic_index_in_dim(pieces, mine ^ step, 0, keepdims=False)
            total = total + lax.ppermute(send, axes, pairs)
        offset = offset * ways + mine
        places.append((bits, mine))
        buffer = total
        if len(places) == tie_after:
            buffer, tie = lax.optimization_barrier((buffer, tie))
    rows = buffer.shape[0]
    position = (offset * rows + lax.broadcasted_iota(jnp.int32, buffer.shape, 0)) * buffer.shape[1]
    position = position + lax.broadcasted_iota(jnp.int32, buffer.shape, 1)
    buffer = buffer * scale_of(position)
    for bits, mine in reversed(places):
        ways = 1 << len(bits)
        both = jnp.zeros((ways,) + buffer.shape, buffer.dtype)
        both = lax.dynamic_update_index_in_dim(both, buffer, mine, 0)
        for step in range(1, ways):
            flip = spread(step, bits)
            pairs = [(i, i ^ flip) for i in range(count)]
            other = lax.ppermute(buffer, axes, pairs)
            both = lax.dynamic_update_index_in_dim(both, other, mine ^ step, 0)
        buffer = both.reshape(-1, buffer.shape[1])
    return buffer, tie


def shards(
    features,
    labels,
    dw_weight,
    dw_bias,
    norm_gain,
    norm_bias,
    w_in,
    b_in,
    w_out,
    b_out,
    layer_scale,
    w_lateral,
    b_lateral,
    w_class,
    b_class,
):
    enc_params = (dw_weight, dw_bias, norm_gain, norm_bias, w_in, b_in, w_out, b_out, layer_scale)
    section = lax.axis_index("section")
    micro_count = features.shape[0]
    height = features.shape[2]
    width = features.shape[3]
    axes = ("section", "row", "col")

    def rimmed(tile):
        return padded_2(tile, (("row", 1), ("col", 2)), 3)

    tile = lax.dynamic_index_in_dim(features, section, 0, keepdims=False)
    label_tile = lax.dynamic_index_in_dim(labels, section, 0, keepdims=False)
    padded = rimmed(tile)
    output, saved = encoder_forward(padded, enc_params)
    returned, loss_sum, dec_grads = decoder(output, label_tile, w_lateral, b_lateral, w_class, b_class)
    d_conv, enc_grads = encoder_backward(saved, returned, enc_params)
    d_padded = rimmed(d_conv)
    d_input, kernel_grad, convbias_grad = conv_backward(padded, d_conv, d_padded, returned, dw_weight)
    (
        gain_grad,
        normbias_grad,
        expand_grad,
        expbias_grad,
        project_grad,
        projbias_grad,
        layerscale_grad,
    ) = enc_grads
    lateral_grad, latbias_grad, classify_grad, clsbias_grad = dec_grads
    vectors = [convbias_grad, gain_grad, normbias_grad, expbias_grad, projbias_grad]
    vectors += [layerscale_grad, latbias_grad, clsbias_grad, loss_sum.reshape(1)]
    joined = jnp.concatenate(vectors)
    parts = [joined, kernel_grad, expand_grad, project_grad, lateral_grad, classify_grad]
    count = math.prod(lax.axis_size(a) for a in axes)
    buffer, shapes = pack_rows(parts, count * 2)
    cell_count = micro_count * height * width * lax.axis_size("row") * lax.axis_size("col")
    grad_scale = 1.0 / math.sqrt(cell_count)
    loss_at = joined.shape[0] - 1

    def scale_of(position):
        return jnp.where(position == loss_at, 1.0 / cell_count, grad_scale).astype(jnp.float32)

    buffer, d_input = butterfly_psum(
        buffer, axes, [(3,), (6, 0), (1, 2), (4, 5)], scale_of, d_input, 2
    )
    joined, kernel_grad, expand_grad, project_grad, lateral_grad, classify_grad = unpack_rows(
        buffer, shapes
    )
    sizes = [v.shape[0] for v in vectors]
    cuts = [sum(sizes[:k]) for k in range(len(sizes) + 1)]
    (
        convbias_grad,
        gain_grad,
        normbias_grad,
        expbias_grad,
        projbias_grad,
        layerscale_grad,
        latbias_grad,
        clsbias_grad,
        loss_total,
    ) = [joined[cuts[k] : cuts[k + 1]] for k in range(len(sizes))]
    return (
        d_input[None],
        loss_total[0],
        kernel_grad,
        convbias_grad,
        gain_grad,
        normbias_grad,
        expand_grad,
        expbias_grad,
        project_grad,
        projbias_grad,
        layerscale_grad,
        lateral_grad,
        latbias_grad,
        classify_grad,
        clsbias_grad,
    )


def solution(mesh):
    placed = (
        P(None, None, "row", "col"),
        P(None, "row", "col"),
        P(),
        P(),
        P(),
        P(),
        P(),
        P(),
        P(),
        P(),
        P(),
        P(),
        P(),
        P(),
        P(),
    )
    return jax.shard_map(
        shards,
        mesh=mesh,
        in_specs=placed,
        out_specs=(
            P("section", None, "row", "col"),
            P(),
            P(),
            P(),
            P(),
            P(),
            P(),
            P(),
            P(),
            P(),
            P(),
            P(),
            P(),
            P(),
            P(),
        ),
        check_vma=False,
    )
```

```python
import math

import jax
import jax.numpy as jnp
from jax import lax
from jax.sharding import PartitionSpec as P

EPSILON = 1e-06
ROOT_HALF = 0.7071067811865476
DENSITY_SCALE = 0.3989422804014327


def padded_2(x, sides, width):
    for axis, dim in sides:
        count, length = (lax.axis_size(axis), x.shape[dim])
        up = [(i, (i + 1) % count) for i in range(count - 1)]
        down = [(j, i) for i, j in up]
        order = (1, 0, 2) if dim == 1 else (2, 1, 0)
        last = jnp.transpose(lax.slice_in_dim(x, length - width, length, axis=dim), order)
        leading = jnp.transpose(lax.slice_in_dim(x, 0, width, axis=dim), order)
        before = jnp.transpose(lax.ppermute(last, axis, up), order)
        after = jnp.transpose(lax.ppermute(leading, axis, down), order)
        x = jnp.concatenate([before, x, after], axis=dim)
    return x


def from_behind(block, axis, distance):
    devices = range(lax.axis_size(axis))
    route = [(i - distance, i) for i in devices if i - distance in devices]
    return lax.ppermute(block, axis, route)


def product(form, left_side, right_side):
    return jnp.einsum(form, left_side, right_side, preferred_element_type=jnp.float32)


def depthwise(padded, kernel, height, width, flipped):
    total = jnp.zeros((padded.shape[0], height, width), jnp.float32)
    for tap_index in range(49):
        down_step = tap_index // 7
        side_step = tap_index % 7
        if flipped:
            down_step = 6 - down_step
            side_step = 6 - side_step
        window = padded[:, down_step : down_step + height, side_step : side_step + width].astype(
            jnp.float32
        )
        total = total + kernel[:, tap_index][:, None, None] * window
    return total


def normal_cdf(values):
    return 0.5 * (1.0 + lax.erf(values * ROOT_HALF))


def gelu_slope(values):
    return normal_cdf(values) + values * jnp.exp(-0.5 * values * values) * DENSITY_SCALE


def encoder_forward(padded, enc_params):
    dw_weight, dw_bias, norm_gain, norm_bias, w_in, b_in, w_out, b_out, layer_scale = enc_params
    height = padded.shape[1] - 6
    width = padded.shape[2] - 6
    conv = depthwise(padded, dw_weight, height, width, False) + dw_bias[:, None, None]
    centre = conv - jnp.mean(conv, axis=0, keepdims=True)
    inv_std = lax.rsqrt(jnp.mean(centre * centre, axis=0, keepdims=True) + EPSILON)
    scaled = centre * inv_std
    normed = (scaled * norm_gain[:, None, None] + norm_bias[:, None, None]).astype(jnp.bfloat16)
    before = product("chw,cd->dhw", normed, w_in) + b_in[:, None, None]
    active = (before * normal_cdf(before)).astype(jnp.bfloat16)
    branch = product("dhw,dc->chw", active, w_out) + b_out[:, None, None]
    inner = padded[:, 3 : 3 + height, 3 : 3 + width].astype(jnp.float32)
    output = (inner + layer_scale[:, None, None] * branch).astype(jnp.bfloat16)
    return (output, (scaled, inv_std, normed, before, active, branch))


def encoder_backward(saved, grad_out, enc_params):
    dw_weight, dw_bias, norm_gain, norm_bias, w_in, b_in, w_out, b_out, layer_scale = enc_params
    scaled, inv_std, normed, before, active, branch = saved
    grad_float = grad_out.astype(jnp.float32)
    layerscale_grad = jnp.sum(branch * grad_float, axis=(1, 2))
    d_branch = (layer_scale[:, None, None] * grad_float).astype(jnp.bfloat16)
    projbias_grad = jnp.sum(d_branch.astype(jnp.float32), axis=(1, 2))
    project_grad = product("dhw,chw->dc", active, d_branch)
    d_active = product("chw,dc->dhw", d_branch, w_out)
    d_before = (d_active * gelu_slope(before)).astype(jnp.bfloat16)
    expbias_grad = jnp.sum(d_before.astype(jnp.float32), axis=(1, 2))
    expand_grad = product("chw,dhw->cd", normed, d_before)
    d_normed = product("dhw,cd->chw", d_before, w_in)
    gain_grad = jnp.sum(d_normed * scaled, axis=(1, 2))
    normbias_grad = jnp.sum(d_normed, axis=(1, 2))
    d_scaled = d_normed * norm_gain[:, None, None]
    d_conv = inv_std * (
        d_scaled
        - jnp.mean(d_scaled, axis=0, keepdims=True)
        - scaled * jnp.mean(d_scaled * scaled, axis=0, keepdims=True)
    )
    grads = (
        gain_grad,
        normbias_grad,
        expand_grad,
        expbias_grad,
        project_grad,
        projbias_grad,
        layerscale_grad,
    )
    return (d_conv.astype(jnp.bfloat16), grads)


def conv_backward(padded, d_conv, d_padded, grad_out, dw_weight):
    height = d_conv.shape[1]
    width = d_conv.shape[2]
    d_input = grad_out.astype(jnp.float32) + depthwise(d_padded, dw_weight, height, width, True)
    conv_float = d_conv.astype(jnp.float32)
    columns = []
    for tap_index in range(49):
        down_step = tap_index // 7
        side_step = tap_index % 7
        window = padded[:, down_step : down_step + height, side_step : side_step + width].astype(
            jnp.float32
        )
        columns.append(jnp.sum(window * conv_float, axis=(1, 2)))
    kernel_grad = jnp.stack(columns, axis=1)
    convbias_grad = jnp.sum(conv_float, axis=(1, 2))
    return (d_input, kernel_grad, convbias_grad)


def decoder(encoded, label_tile, w_lateral, b_lateral, w_class, b_class):
    lateral_pre = product("chw,cl->lhw", encoded, w_lateral) + b_lateral[:, None, None]
    lateral = (lateral_pre * normal_cdf(lateral_pre)).astype(jnp.bfloat16)
    logits = product("lhw,lk->khw", lateral, w_class) + b_class[:, None, None]
    highest = jnp.max(logits, axis=0, keepdims=True)
    shifted = logits - highest
    totals = jnp.sum(jnp.exp(shifted), axis=0, keepdims=True)
    log_total = highest + jnp.log(totals)
    classes = jnp.arange(logits.shape[0], dtype=jnp.int32)
    onehot = (label_tile[None, :, :] == classes[:, None, None]).astype(jnp.float32)
    loss_sum = jnp.sum(log_total[0] - jnp.sum(onehot * logits, axis=0))
    d_logits = (jnp.exp(shifted) / totals - onehot).astype(jnp.bfloat16)
    classify_grad = product("lhw,khw->lk", lateral, d_logits)
    clsbias_grad = jnp.sum(d_logits.astype(jnp.float32), axis=(1, 2))
    d_lateral_raw = product("khw,lk->lhw", d_logits, w_class)
    d_lateral = (d_lateral_raw * gelu_slope(lateral_pre)).astype(jnp.bfloat16)
    lateral_grad = product("chw,lhw->cl", encoded, d_lateral)
    latbias_grad = jnp.sum(d_lateral.astype(jnp.float32), axis=(1, 2))
    d_encoded = product("lhw,cl->chw", d_lateral, w_lateral).astype(jnp.bfloat16)
    return (d_encoded, loss_sum, (lateral_grad, latbias_grad, classify_grad, clsbias_grad))


LANES = 128


def pack_rows(parts, multiple):
    shapes, rows = [], []
    for part in parts:
        flat = part.reshape(-1)
        size = flat.shape[0]
        padded_rows = -(-size // (8 * LANES)) * 8
        flat = jnp.pad(flat, (0, padded_rows * LANES - size))
        rows.append(flat.reshape(padded_rows, LANES))
        shapes.append(part.shape)
    total = sum(r.shape[0] for r in rows)
    extra = -total % multiple
    if extra:
        rows.append(jnp.zeros((extra, LANES), jnp.float32))
    return jnp.concatenate(rows, axis=0), shapes


def unpack_rows(buffer, shapes):
    out, at = [], 0
    for shape in shapes:
        size = math.prod(shape)
        padded_rows = -(-size // (8 * LANES)) * 8
        out.append(buffer[at : at + padded_rows].reshape(-1)[:size].reshape(shape))
        at += padded_rows
    return out


def spread(value, bits):
    out = 0
    for k, bit_at in enumerate(bits):
        if (value >> k) & 1:
            out |= 1 << bit_at
    return out


def butterfly_psum(buffer, axes, stages, scale_of, tie, tie_after):
    index = lax.axis_index(axes)
    count = math.prod(lax.axis_size(a) for a in axes)
    offset = jnp.zeros((), jnp.int32)
    places = []
    for bits in stages:
        ways = 1 << len(bits)
        mine = sum(((index >> bit_at) & 1) << k for k, bit_at in enumerate(bits))
        pieces = buffer.reshape(ways, buffer.shape[0] // ways, buffer.shape[1])
        total = lax.dynamic_index_in_dim(pieces, mine, 0, keepdims=False)
        for step in range(1, ways):
            flip = spread(step, bits)
            pairs = [(i, i ^ flip) for i in range(count)]
            send = lax.dynamic_index_in_dim(pieces, mine ^ step, 0, keepdims=False)
            total = total + lax.ppermute(send, axes, pairs)
        offset = offset * ways + mine
        places.append((bits, mine))
        buffer = total
        if len(places) == tie_after:
            buffer, tie = lax.optimization_barrier((buffer, tie))
    rows = buffer.shape[0]
    position = (offset * rows + lax.broadcasted_iota(jnp.int32, buffer.shape, 0)) * buffer.shape[1]
    position = position + lax.broadcasted_iota(jnp.int32, buffer.shape, 1)
    buffer = buffer * scale_of(position)
    for bits, mine in reversed(places):
        ways = 1 << len(bits)
        both = jnp.zeros((ways,) + buffer.shape, buffer.dtype)
        both = lax.dynamic_update_index_in_dim(both, buffer, mine, 0)
        for step in range(1, ways):
            flip = spread(step, bits)
            pairs = [(i, i ^ flip) for i in range(count)]
            other = lax.ppermute(buffer, axes, pairs)
            both = lax.dynamic_update_index_in_dim(both, other, mine ^ step, 0)
        buffer = both.reshape(-1, buffer.shape[1])
    return buffer, tie


def shards(
    features,
    labels,
    dw_weight,
    dw_bias,
    norm_gain,
    norm_bias,
    w_in,
    b_in,
    w_out,
    b_out,
    layer_scale,
    w_lateral,
    b_lateral,
    w_class,
    b_class,
):
    enc_params = (dw_weight, dw_bias, norm_gain, norm_bias, w_in, b_in, w_out, b_out, layer_scale)
    section = lax.axis_index("section")
    micro_count = features.shape[0]
    height = features.shape[2]
    width = features.shape[3]
    axes = ("section", "row", "col")

    def rimmed(tile):
        return padded_2(tile, (("row", 1), ("col", 2)), 3)

    tile = lax.dynamic_index_in_dim(features, section, 0, keepdims=False)
    label_tile = lax.dynamic_index_in_dim(labels, section, 0, keepdims=False)
    padded = rimmed(tile)
    output, saved = encoder_forward(padded, enc_params)
    returned, loss_sum, dec_grads = decoder(output, label_tile, w_lateral, b_lateral, w_class, b_class)
    d_conv, enc_grads = encoder_backward(saved, returned, enc_params)
    d_padded = rimmed(d_conv)
    d_input, kernel_grad, convbias_grad = conv_backward(padded, d_conv, d_padded, returned, dw_weight)
    (
        gain_grad,
        normbias_grad,
        expand_grad,
        expbias_grad,
        project_grad,
        projbias_grad,
        layerscale_grad,
    ) = enc_grads
    lateral_grad, latbias_grad, classify_grad, clsbias_grad = dec_grads
    vectors = [convbias_grad, gain_grad, normbias_grad, expbias_grad, projbias_grad]
    vectors += [layerscale_grad, latbias_grad, clsbias_grad, loss_sum.reshape(1)]
    joined = jnp.concatenate(vectors)
    parts = [joined, kernel_grad, expand_grad, project_grad, lateral_grad, classify_grad]
    count = math.prod(lax.axis_size(a) for a in axes)
    buffer, shapes = pack_rows(parts, count * 2)
    cell_count = micro_count * height * width * lax.axis_size("row") * lax.axis_size("col")
    grad_scale = 1.0 / math.sqrt(cell_count)
    loss_at = joined.shape[0] - 1

    def scale_of(position):
        return jnp.where(position == loss_at, 1.0 / cell_count, grad_scale).astype(jnp.float32)

    buffer, d_input = butterfly_psum(
        buffer, axes, [(3,), (6, 0), (1, 2), (4, 5)], scale_of, d_input, 2
    )
    joined, kernel_grad, expand_grad, project_grad, lateral_grad, classify_grad = unpack_rows(
        buffer, shapes
    )
    sizes = [v.shape[0] for v in vectors]
    cuts = [sum(sizes[:k]) for k in range(len(sizes) + 1)]
    (
        convbias_grad,
        gain_grad,
        normbias_grad,
        expbias_grad,
        projbias_grad,
        layerscale_grad,
        latbias_grad,
        clsbias_grad,
        loss_total,
    ) = [joined[cuts[k] : cuts[k + 1]] for k in range(len(sizes))]
    return (
        d_input[None],
        loss_total[0],
        kernel_grad,
        convbias_grad,
        gain_grad,
        normbias_grad,
        expand_grad,
        expbias_grad,
        project_grad,
        projbias_grad,
        layerscale_grad,
        lateral_grad,
        latbias_grad,
        classify_grad,
        clsbias_grad,
    )


def solution(mesh):
    placed = (
        P(None, None, "row", "col"),
        P(None, "row", "col"),
        P(),
        P(),
        P(),
        P(),
        P(),
        P(),
        P(),
        P(),
        P(),
        P(),
        P(),
        P(),
        P(),
    )
    return jax.shard_map(
        shards,
        mesh=mesh,
        in_specs=placed,
        out_specs=(
            P("section", None, "row", "col"),
            P(),
            P(),
            P(),
            P(),
            P(),
            P(),
            P(),
            P(),
            P(),
            P(),
            P(),
            P(),
            P(),
            P(),
        ),
        check_vma=False,
    )
```

```python
import math

import jax
import jax.numpy as jnp
from jax import lax
from jax.sharding import PartitionSpec as P

EPSILON = 1e-06
ROOT_HALF = 0.7071067811865476
DENSITY_SCALE = 0.3989422804014327


def padded_2(x, sides, width):
    for axis, dim in sides:
        count, length = (lax.axis_size(axis), x.shape[dim])
        up = [(i, (i + 1) % count) for i in range(count - 1)]
        down = [(j, i) for i, j in up]
        order = (1, 0, 2) if dim == 1 else (2, 1, 0)
        last = jnp.transpose(lax.slice_in_dim(x, length - width, length, axis=dim), order)
        leading = jnp.transpose(lax.slice_in_dim(x, 0, width, axis=dim), order)
        before = jnp.transpose(lax.ppermute(last, axis, up), order)
        after = jnp.transpose(lax.ppermute(leading, axis, down), order)
        x = jnp.concatenate([before, x, after], axis=dim)
    return x


def from_behind(block, axis, distance):
    devices = range(lax.axis_size(axis))
    route = [(i - distance, i) for i in devices if i - distance in devices]
    return lax.ppermute(block, axis, route)


def product(form, left_side, right_side):
    return jnp.einsum(form, left_side, right_side, preferred_element_type=jnp.float32)


def depthwise(padded, kernel, height, width, flipped):
    total = jnp.zeros((padded.shape[0], height, width), jnp.float32)
    for tap_index in range(49):
        down_step = tap_index // 7
        side_step = tap_index % 7
        if flipped:
            down_step = 6 - down_step
            side_step = 6 - side_step
        window = padded[:, down_step : down_step + height, side_step : side_step + width].astype(
            jnp.float32
        )
        total = total + kernel[:, tap_index][:, None, None] * window
    return total


def normal_cdf(values):
    return 0.5 * (1.0 + lax.erf(values * ROOT_HALF))


def gelu_slope(values):
    return normal_cdf(values) + values * jnp.exp(-0.5 * values * values) * DENSITY_SCALE


def encoder_forward(padded, enc_params):
    dw_weight, dw_bias, norm_gain, norm_bias, w_in, b_in, w_out, b_out, layer_scale = enc_params
    height = padded.shape[1] - 6
    width = padded.shape[2] - 6
    conv = depthwise(padded, dw_weight, height, width, False) + dw_bias[:, None, None]
    centre = conv - jnp.mean(conv, axis=0, keepdims=True)
    inv_std = lax.rsqrt(jnp.mean(centre * centre, axis=0, keepdims=True) + EPSILON)
    scaled = centre * inv_std
    normed = (scaled * norm_gain[:, None, None] + norm_bias[:, None, None]).astype(jnp.bfloat16)
    before = product("chw,cd->dhw", normed, w_in) + b_in[:, None, None]
    active = (before * normal_cdf(before)).astype(jnp.bfloat16)
    branch = product("dhw,dc->chw", active, w_out) + b_out[:, None, None]
    inner = padded[:, 3 : 3 + height, 3 : 3 + width].astype(jnp.float32)
    output = (inner + layer_scale[:, None, None] * branch).astype(jnp.bfloat16)
    return (output, (scaled, inv_std, normed, before, active, branch))


def encoder_backward(saved, grad_out, enc_params):
    dw_weight, dw_bias, norm_gain, norm_bias, w_in, b_in, w_out, b_out, layer_scale = enc_params
    scaled, inv_std, normed, before, active, branch = saved
    grad_float = grad_out.astype(jnp.float32)
    layerscale_grad = jnp.sum(branch * grad_float, axis=(1, 2))
    d_branch = (layer_scale[:, None, None] * grad_float).astype(jnp.bfloat16)
    projbias_grad = jnp.sum(d_branch.astype(jnp.float32), axis=(1, 2))
    project_grad = product("dhw,chw->dc", active, d_branch)
    d_active = product("chw,dc->dhw", d_branch, w_out)
    d_before = (d_active * gelu_slope(before)).astype(jnp.bfloat16)
    expbias_grad = jnp.sum(d_before.astype(jnp.float32), axis=(1, 2))
    expand_grad = product("chw,dhw->cd", normed, d_before)
    d_normed = product("dhw,cd->chw", d_before, w_in)
    gain_grad = jnp.sum(d_normed * scaled, axis=(1, 2))
    normbias_grad = jnp.sum(d_normed, axis=(1, 2))
    d_scaled = d_normed * norm_gain[:, None, None]
    d_conv = inv_std * (
        d_scaled
        - jnp.mean(d_scaled, axis=0, keepdims=True)
        - scaled * jnp.mean(d_scaled * scaled, axis=0, keepdims=True)
    )
    grads = (
        gain_grad,
        normbias_grad,
        expand_grad,
        expbias_grad,
        project_grad,
        projbias_grad,
        layerscale_grad,
    )
    return (d_conv.astype(jnp.bfloat16), grads)


def conv_backward(padded, d_conv, d_padded, grad_out, dw_weight):
    height = d_conv.shape[1]
    width = d_conv.shape[2]
    d_input = grad_out.astype(jnp.float32) + depthwise(d_padded, dw_weight, height, width, True)
    conv_float = d_conv.astype(jnp.float32)
    columns = []
    for tap_index in range(49):
        down_step = tap_index // 7
        side_step = tap_index % 7
        window = padded[:, down_step : down_step + height, side_step : side_step + width].astype(
            jnp.float32
        )
        columns.append(jnp.sum(window * conv_float, axis=(1, 2)))
    kernel_grad = jnp.stack(columns, axis=1)
    convbias_grad = jnp.sum(conv_float, axis=(1, 2))
    return (d_input, kernel_grad, convbias_grad)


def decoder(encoded, label_tile, w_lateral, b_lateral, w_class, b_class):
    lateral_pre = product("chw,cl->lhw", encoded, w_lateral) + b_lateral[:, None, None]
    lateral = (lateral_pre * normal_cdf(lateral_pre)).astype(jnp.bfloat16)
    logits = product("lhw,lk->khw", lateral, w_class) + b_class[:, None, None]
    highest = jnp.max(logits, axis=0, keepdims=True)
    shifted = logits - highest
    totals = jnp.sum(jnp.exp(shifted), axis=0, keepdims=True)
    log_total = highest + jnp.log(totals)
    classes = jnp.arange(logits.shape[0], dtype=jnp.int32)
    onehot = (label_tile[None, :, :] == classes[:, None, None]).astype(jnp.float32)
    loss_sum = jnp.sum(log_total[0] - jnp.sum(onehot * logits, axis=0))
    d_logits = (jnp.exp(shifted) / totals - onehot).astype(jnp.bfloat16)
    classify_grad = product("lhw,khw->lk", lateral, d_logits)
    clsbias_grad = jnp.sum(d_logits.astype(jnp.float32), axis=(1, 2))
    d_lateral_raw = product("khw,lk->lhw", d_logits, w_class)
    d_lateral = (d_lateral_raw * gelu_slope(lateral_pre)).astype(jnp.bfloat16)
    lateral_grad = product("chw,lhw->cl", encoded, d_lateral)
    latbias_grad = jnp.sum(d_lateral.astype(jnp.float32), axis=(1, 2))
    d_encoded = product("lhw,cl->chw", d_lateral, w_lateral).astype(jnp.bfloat16)
    return (d_encoded, loss_sum, (lateral_grad, latbias_grad, classify_grad, clsbias_grad))


LANES = 128


def tile_order(x):
    rows, cols = x.shape
    x = x.reshape(rows // 8, 8, cols // LANES, LANES).transpose(0, 2, 1, 3)
    return x.reshape(rows * cols // LANES, LANES)


def from_tile_order(x, shape):
    rows, cols = shape
    x = x.reshape(rows // 8, cols // LANES, 8, LANES).transpose(0, 2, 1, 3)
    return x.reshape(rows, cols)


def tiled(shape):
    return len(shape) == 2 and shape[0] % 8 == 0 and shape[1] % LANES == 0


def pack_rows(parts, multiple):
    shapes, rows = [], []
    for part in parts:
        shapes.append(part.shape)
        if tiled(part.shape):
            rows.append(tile_order(part))
            continue
        flat = part.reshape(-1)
        size = flat.shape[0]
        padded_rows = -(-size // (8 * LANES)) * 8
        flat = jnp.pad(flat, (0, padded_rows * LANES - size))
        rows.append(flat.reshape(padded_rows, LANES))
    total = sum(r.shape[0] for r in rows)
    extra = -total % multiple
    if extra:
        rows.append(jnp.zeros((extra, LANES), jnp.float32))
    return jnp.concatenate(rows, axis=0), shapes


def unpack_rows(buffer, shapes):
    out, at = [], 0
    for shape in shapes:
        size = math.prod(shape)
        padded_rows = -(-size // (8 * LANES)) * 8
        piece = buffer[at : at + padded_rows]
        if tiled(shape):
            out.append(from_tile_order(piece, shape))
        else:
            out.append(piece.reshape(-1)[:size].reshape(shape))
        at += padded_rows
    return out


def spread(value, bits):
    out = 0
    for k, bit_at in enumerate(bits):
        if (value >> k) & 1:
            out |= 1 << bit_at
    return out


def butterfly_psum(buffer, axes, stages, scale_of, tie, tie_after):
    index = lax.axis_index(axes)
    count = math.prod(lax.axis_size(a) for a in axes)
    offset = jnp.zeros((), jnp.int32)
    places = []
    for bits in stages:
        ways = 1 << len(bits)
        mine = sum(((index >> bit_at) & 1) << k for k, bit_at in enumerate(bits))
        pieces = buffer.reshape(ways, buffer.shape[0] // ways, buffer.shape[1])
        total = lax.dynamic_index_in_dim(pieces, mine, 0, keepdims=False)
        for step in range(1, ways):
            flip = spread(step, bits)
            pairs = [(i, i ^ flip) for i in range(count)]
            send = lax.dynamic_index_in_dim(pieces, mine ^ step, 0, keepdims=False)
            total = total + lax.ppermute(send, axes, pairs)
        offset = offset * ways + mine
        places.append((bits, mine))
        buffer = total
        if len(places) == tie_after:
            buffer, tie = lax.optimization_barrier((buffer, tie))
    rows = buffer.shape[0]
    position = (offset * rows + lax.broadcasted_iota(jnp.int32, buffer.shape, 0)) * buffer.shape[1]
    position = position + lax.broadcasted_iota(jnp.int32, buffer.shape, 1)
    buffer = buffer * scale_of(position)
    for bits, mine in reversed(places):
        ways = 1 << len(bits)
        both = jnp.zeros((ways,) + buffer.shape, buffer.dtype)
        both = lax.dynamic_update_index_in_dim(both, buffer, mine, 0)
        for step in range(1, ways):
            flip = spread(step, bits)
            pairs = [(i, i ^ flip) for i in range(count)]
            other = lax.ppermute(buffer, axes, pairs)
            both = lax.dynamic_update_index_in_dim(both, other, mine ^ step, 0)
        buffer = both.reshape(-1, buffer.shape[1])
    return buffer, tie


def shards(
    features,
    labels,
    dw_weight,
    dw_bias,
    norm_gain,
    norm_bias,
    w_in,
    b_in,
    w_out,
    b_out,
    layer_scale,
    w_lateral,
    b_lateral,
    w_class,
    b_class,
):
    enc_params = (dw_weight, dw_bias, norm_gain, norm_bias, w_in, b_in, w_out, b_out, layer_scale)
    section = lax.axis_index("section")
    micro_count = features.shape[0]
    height = features.shape[2]
    width = features.shape[3]
    axes = ("section", "row", "col")

    def rimmed(tile):
        return padded_2(tile, (("row", 1), ("col", 2)), 3)

    tile = lax.dynamic_index_in_dim(features, section, 0, keepdims=False)
    label_tile = lax.dynamic_index_in_dim(labels, section, 0, keepdims=False)
    padded = rimmed(tile)
    output, saved = encoder_forward(padded, enc_params)
    returned, loss_sum, dec_grads = decoder(output, label_tile, w_lateral, b_lateral, w_class, b_class)
    d_conv, enc_grads = encoder_backward(saved, returned, enc_params)
    d_padded = rimmed(d_conv)
    d_input, kernel_grad, convbias_grad = conv_backward(padded, d_conv, d_padded, returned, dw_weight)
    (
        gain_grad,
        normbias_grad,
        expand_grad,
        expbias_grad,
        project_grad,
        projbias_grad,
        layerscale_grad,
    ) = enc_grads
    lateral_grad, latbias_grad, classify_grad, clsbias_grad = dec_grads
    vectors = [convbias_grad, gain_grad, normbias_grad, expbias_grad, projbias_grad]
    vectors += [layerscale_grad, latbias_grad, clsbias_grad, loss_sum.reshape(1)]
    joined = jnp.concatenate(vectors)
    parts = [joined, kernel_grad, expand_grad, project_grad.T, lateral_grad, classify_grad]
    count = math.prod(lax.axis_size(a) for a in axes)
    buffer, shapes = pack_rows(parts, count * 2)
    cell_count = micro_count * height * width * lax.axis_size("row") * lax.axis_size("col")
    grad_scale = 1.0 / math.sqrt(cell_count)
    loss_at = joined.shape[0] - 1

    def scale_of(position):
        return jnp.where(position == loss_at, 1.0 / cell_count, grad_scale).astype(jnp.float32)

    buffer, d_input = butterfly_psum(
        buffer, axes, [(3,), (6, 0), (1, 2), (4, 5)], scale_of, d_input, 2
    )
    joined, kernel_grad, expand_grad, project_grad, lateral_grad, classify_grad = unpack_rows(
        buffer, shapes
    )
    project_grad = project_grad.T
    sizes = [v.shape[0] for v in vectors]
    cuts = [sum(sizes[:k]) for k in range(len(sizes) + 1)]
    (
        convbias_grad,
        gain_grad,
        normbias_grad,
        expbias_grad,
        projbias_grad,
        layerscale_grad,
        latbias_grad,
        clsbias_grad,
        loss_total,
    ) = [joined[cuts[k] : cuts[k + 1]] for k in range(len(sizes))]
    return (
        d_input[None],
        loss_total[0],
        kernel_grad,
        convbias_grad,
        gain_grad,
        normbias_grad,
        expand_grad,
        expbias_grad,
        project_grad,
        projbias_grad,
        layerscale_grad,
        lateral_grad,
        latbias_grad,
        classify_grad,
        clsbias_grad,
    )


def solution(mesh):
    placed = (
        P(None, None, "row", "col"),
        P(None, "row", "col"),
        P(),
        P(),
        P(),
        P(),
        P(),
        P(),
        P(),
        P(),
        P(),
        P(),
        P(),
        P(),
        P(),
    )
    return jax.shard_map(
        shards,
        mesh=mesh,
        in_specs=placed,
        out_specs=(
            P("section", None, "row", "col"),
            P(),
            P(),
            P(),
            P(),
            P(),
            P(),
            P(),
            P(),
            P(),
            P(),
            P(),
            P(),
            P(),
            P(),
        ),
        check_vma=False,
    )
```

```python
import math

import jax
import jax.numpy as jnp
from jax import lax
from jax.sharding import PartitionSpec as P

EPSILON = 1e-06
ROOT_HALF = 0.7071067811865476
DENSITY_SCALE = 0.3989422804014327


def padded_2(x, sides, width):
    (row_axis, row_dim), (col_axis, col_dim) = sides
    rows, cols = lax.axis_size(row_axis), lax.axis_size(col_axis)
    height, length = x.shape[row_dim], x.shape[col_dim]
    both = (row_axis, col_axis)

    def moved(block, dr, dc, order):
        pairs = []
        for r in range(rows):
            for c in range(cols):
                if 0 <= r + dr < rows and 0 <= c + dc < cols:
                    pairs.append((r * cols + c, (r + dr) * cols + c + dc))
        block = jnp.transpose(block, order)
        if dc == 0:
            sent = lax.ppermute(block, row_axis, [(a // cols, b // cols) for a, b in pairs[::cols]])
        elif dr == 0:
            sent = lax.ppermute(block, col_axis, [(a % cols, b % cols) for a, b in pairs[:cols - 1]])
        else:
            sent = lax.ppermute(block, both, pairs)
        return jnp.transpose(sent, order)

    top = lax.slice_in_dim(x, 0, width, axis=row_dim)
    bottom = lax.slice_in_dim(x, height - width, height, axis=row_dim)
    left = lax.slice_in_dim(x, 0, width, axis=col_dim)
    right = lax.slice_in_dim(x, length - width, length, axis=col_dim)
    strips = (1, 0, 2)
    thin = (2, 1, 0)
    above = moved(bottom, 1, 0, strips)
    below = moved(top, -1, 0, strips)
    before = moved(right, 0, 1, thin)
    after = moved(left, 0, -1, thin)

    def corner(block_rows, block_cols, dr, dc):
        block = lax.slice_in_dim(lax.slice_in_dim(x, *block_rows, axis=row_dim), *block_cols, axis=col_dim)
        return moved(block, dr, dc, thin)

    low, high = (0, width), (height - width, height)
    first, last = (0, width), (length - width, length)
    above_before = corner(high, last, 1, 1)
    above_after = corner(high, first, 1, -1)
    below_before = corner(low, last, -1, 1)
    below_after = corner(low, first, -1, -1)
    upper = jnp.concatenate([above_before, above, above_after], axis=col_dim)
    middle = jnp.concatenate([before, x, after], axis=col_dim)
    lower = jnp.concatenate([below_before, below, below_after], axis=col_dim)
    return jnp.concatenate([upper, middle, lower], axis=row_dim)


def from_behind(block, axis, distance):
    devices = range(lax.axis_size(axis))
    route = [(i - distance, i) for i in devices if i - distance in devices]
    return lax.ppermute(block, axis, route)


def product(form, left_side, right_side):
    return jnp.einsum(form, left_side, right_side, preferred_element_type=jnp.float32)


def depthwise(padded, kernel, height, width, flipped):
    total = jnp.zeros((padded.shape[0], height, width), jnp.float32)
    for tap_index in range(49):
        down_step = tap_index // 7
        side_step = tap_index % 7
        if flipped:
            down_step = 6 - down_step
            side_step = 6 - side_step
        window = padded[:, down_step : down_step + height, side_step : side_step + width].astype(
            jnp.float32
        )
        total = total + kernel[:, tap_index][:, None, None] * window
    return total


def normal_cdf(values):
    return 0.5 * (1.0 + lax.erf(values * ROOT_HALF))


def gelu_slope(values):
    return normal_cdf(values) + values * jnp.exp(-0.5 * values * values) * DENSITY_SCALE


def encoder_forward(padded, enc_params):
    dw_weight, dw_bias, norm_gain, norm_bias, w_in, b_in, w_out, b_out, layer_scale = enc_params
    height = padded.shape[1] - 6
    width = padded.shape[2] - 6
    conv = depthwise(padded, dw_weight, height, width, False) + dw_bias[:, None, None]
    centre = conv - jnp.mean(conv, axis=0, keepdims=True)
    inv_std = lax.rsqrt(jnp.mean(centre * centre, axis=0, keepdims=True) + EPSILON)
    scaled = centre * inv_std
    normed = (scaled * norm_gain[:, None, None] + norm_bias[:, None, None]).astype(jnp.bfloat16)
    before = product("chw,cd->dhw", normed, w_in) + b_in[:, None, None]
    active = (before * normal_cdf(before)).astype(jnp.bfloat16)
    branch = product("dhw,dc->chw", active, w_out) + b_out[:, None, None]
    inner = padded[:, 3 : 3 + height, 3 : 3 + width].astype(jnp.float32)
    output = (inner + layer_scale[:, None, None] * branch).astype(jnp.bfloat16)
    return (output, (scaled, inv_std, normed, before, active, branch))


def encoder_backward(saved, grad_out, enc_params):
    dw_weight, dw_bias, norm_gain, norm_bias, w_in, b_in, w_out, b_out, layer_scale = enc_params
    scaled, inv_std, normed, before, active, branch = saved
    grad_float = grad_out.astype(jnp.float32)
    layerscale_grad = jnp.sum(branch * grad_float, axis=(1, 2))
    d_branch = (layer_scale[:, None, None] * grad_float).astype(jnp.bfloat16)
    projbias_grad = jnp.sum(d_branch.astype(jnp.float32), axis=(1, 2))
    project_grad = product("dhw,chw->dc", active, d_branch)
    d_active = product("chw,dc->dhw", d_branch, w_out)
    d_before = (d_active * gelu_slope(before)).astype(jnp.bfloat16)
    expbias_grad = jnp.sum(d_before.astype(jnp.float32), axis=(1, 2))
    expand_grad = product("chw,dhw->cd", normed, d_before)
    d_normed = product("dhw,cd->chw", d_before, w_in)
    gain_grad = jnp.sum(d_normed * scaled, axis=(1, 2))
    normbias_grad = jnp.sum(d_normed, axis=(1, 2))
    d_scaled = d_normed * norm_gain[:, None, None]
    d_conv = inv_std * (
        d_scaled
        - jnp.mean(d_scaled, axis=0, keepdims=True)
        - scaled * jnp.mean(d_scaled * scaled, axis=0, keepdims=True)
    )
    grads = (
        gain_grad,
        normbias_grad,
        expand_grad,
        expbias_grad,
        project_grad,
        projbias_grad,
        layerscale_grad,
    )
    return (d_conv.astype(jnp.bfloat16), grads)


def conv_backward(padded, d_conv, d_padded, grad_out, dw_weight):
    height = d_conv.shape[1]
    width = d_conv.shape[2]
    d_input = grad_out.astype(jnp.float32) + depthwise(d_padded, dw_weight, height, width, True)
    conv_float = d_conv.astype(jnp.float32)
    columns = []
    for tap_index in range(49):
        down_step = tap_index // 7
        side_step = tap_index % 7
        window = padded[:, down_step : down_step + height, side_step : side_step + width].astype(
            jnp.float32
        )
        columns.append(jnp.sum(window * conv_float, axis=(1, 2)))
    kernel_grad = jnp.stack(columns, axis=1)
    convbias_grad = jnp.sum(conv_float, axis=(1, 2))
    return (d_input, kernel_grad, convbias_grad)


def decoder(encoded, label_tile, w_lateral, b_lateral, w_class, b_class):
    lateral_pre = product("chw,cl->lhw", encoded, w_lateral) + b_lateral[:, None, None]
    lateral = (lateral_pre * normal_cdf(lateral_pre)).astype(jnp.bfloat16)
    logits = product("lhw,lk->khw", lateral, w_class) + b_class[:, None, None]
    highest = jnp.max(logits, axis=0, keepdims=True)
    shifted = logits - highest
    totals = jnp.sum(jnp.exp(shifted), axis=0, keepdims=True)
    log_total = highest + jnp.log(totals)
    classes = jnp.arange(logits.shape[0], dtype=jnp.int32)
    onehot = (label_tile[None, :, :] == classes[:, None, None]).astype(jnp.float32)
    loss_sum = jnp.sum(log_total[0] - jnp.sum(onehot * logits, axis=0))
    d_logits = (jnp.exp(shifted) / totals - onehot).astype(jnp.bfloat16)
    classify_grad = product("lhw,khw->lk", lateral, d_logits)
    clsbias_grad = jnp.sum(d_logits.astype(jnp.float32), axis=(1, 2))
    d_lateral_raw = product("khw,lk->lhw", d_logits, w_class)
    d_lateral = (d_lateral_raw * gelu_slope(lateral_pre)).astype(jnp.bfloat16)
    lateral_grad = product("chw,lhw->cl", encoded, d_lateral)
    latbias_grad = jnp.sum(d_lateral.astype(jnp.float32), axis=(1, 2))
    d_encoded = product("lhw,cl->chw", d_lateral, w_lateral).astype(jnp.bfloat16)
    return (d_encoded, loss_sum, (lateral_grad, latbias_grad, classify_grad, clsbias_grad))


LANES = 128


def tile_order(x):
    rows, cols = x.shape
    x = x.reshape(rows // 8, 8, cols // LANES, LANES).transpose(0, 2, 1, 3)
    return x.reshape(rows * cols // LANES, LANES)


def from_tile_order(x, shape):
    rows, cols = shape
    x = x.reshape(rows // 8, cols // LANES, 8, LANES).transpose(0, 2, 1, 3)
    return x.reshape(rows, cols)


def tiled(shape):
    return len(shape) == 2 and shape[0] % 8 == 0 and shape[1] % LANES == 0


def pack_rows(parts, multiple):
    shapes, rows = [], []
    for part in parts:
        shapes.append(part.shape)
        if tiled(part.shape):
            rows.append(tile_order(part))
            continue
        flat = part.reshape(-1)
        size = flat.shape[0]
        padded_rows = -(-size // (8 * LANES)) * 8
        flat = jnp.pad(flat, (0, padded_rows * LANES - size))
        rows.append(flat.reshape(padded_rows, LANES))
    total = sum(r.shape[0] for r in rows)
    extra = -total % multiple
    if extra:
        rows.append(jnp.zeros((extra, LANES), jnp.float32))
    return jnp.concatenate(rows, axis=0), shapes


def unpack_rows(buffer, shapes):
    out, at = [], 0
    for shape in shapes:
        size = math.prod(shape)
        padded_rows = -(-size // (8 * LANES)) * 8
        piece = buffer[at : at + padded_rows]
        if tiled(shape):
            out.append(from_tile_order(piece, shape))
        else:
            out.append(piece.reshape(-1)[:size].reshape(shape))
        at += padded_rows
    return out


def spread(value, bits):
    out = 0
    for k, bit_at in enumerate(bits):
        if (value >> k) & 1:
            out |= 1 << bit_at
    return out


def butterfly_psum(buffer, axes, stages, scale_of, tie, tie_after):
    index = lax.axis_index(axes)
    count = math.prod(lax.axis_size(a) for a in axes)
    offset = jnp.zeros((), jnp.int32)
    places = []
    for bits in stages:
        ways = 1 << len(bits)
        mine = sum(((index >> bit_at) & 1) << k for k, bit_at in enumerate(bits))
        pieces = buffer.reshape(ways, buffer.shape[0] // ways, buffer.shape[1])
        total = lax.dynamic_index_in_dim(pieces, mine, 0, keepdims=False)
        for step in range(1, ways):
            flip = spread(step, bits)
            pairs = [(i, i ^ flip) for i in range(count)]
            send = lax.dynamic_index_in_dim(pieces, mine ^ step, 0, keepdims=False)
            total = total + lax.ppermute(send, axes, pairs)
        offset = offset * ways + mine
        places.append((bits, mine))
        buffer = total
        if len(places) == tie_after:
            buffer, tie = lax.optimization_barrier((buffer, tie))
    rows = buffer.shape[0]
    position = (offset * rows + lax.broadcasted_iota(jnp.int32, buffer.shape, 0)) * buffer.shape[1]
    position = position + lax.broadcasted_iota(jnp.int32, buffer.shape, 1)
    buffer = buffer * scale_of(position)
    for bits, mine in reversed(places):
        ways = 1 << len(bits)
        both = jnp.zeros((ways,) + buffer.shape, buffer.dtype)
        both = lax.dynamic_update_index_in_dim(both, buffer, mine, 0)
        for step in range(1, ways):
            flip = spread(step, bits)
            pairs = [(i, i ^ flip) for i in range(count)]
            other = lax.ppermute(buffer, axes, pairs)
            both = lax.dynamic_update_index_in_dim(both, other, mine ^ step, 0)
        buffer = both.reshape(-1, buffer.shape[1])
    return buffer, tie


def shards(
    features,
    labels,
    dw_weight,
    dw_bias,
    norm_gain,
    norm_bias,
    w_in,
    b_in,
    w_out,
    b_out,
    layer_scale,
    w_lateral,
    b_lateral,
    w_class,
    b_class,
):
    enc_params = (dw_weight, dw_bias, norm_gain, norm_bias, w_in, b_in, w_out, b_out, layer_scale)
    section = lax.axis_index("section")
    micro_count = features.shape[0]
    height = features.shape[2]
    width = features.shape[3]
    axes = ("section", "row", "col")

    def rimmed(tile):
        return padded_2(tile, (("row", 1), ("col", 2)), 3)

    tile = lax.dynamic_index_in_dim(features, section, 0, keepdims=False)
    label_tile = lax.dynamic_index_in_dim(labels, section, 0, keepdims=False)
    padded = rimmed(tile)
    output, saved = encoder_forward(padded, enc_params)
    returned, loss_sum, dec_grads = decoder(output, label_tile, w_lateral, b_lateral, w_class, b_class)
    d_conv, enc_grads = encoder_backward(saved, returned, enc_params)
    d_padded = rimmed(d_conv)
    d_input, kernel_grad, convbias_grad = conv_backward(padded, d_conv, d_padded, returned, dw_weight)
    (
        gain_grad,
        normbias_grad,
        expand_grad,
        expbias_grad,
        project_grad,
        projbias_grad,
        layerscale_grad,
    ) = enc_grads
    lateral_grad, latbias_grad, classify_grad, clsbias_grad = dec_grads
    vectors = [convbias_grad, gain_grad, normbias_grad, expbias_grad, projbias_grad]
    vectors += [layerscale_grad, latbias_grad, clsbias_grad, loss_sum.reshape(1)]
    joined = jnp.concatenate(vectors)
    parts = [joined, kernel_grad, expand_grad, project_grad.T, lateral_grad, classify_grad]
    count = math.prod(lax.axis_size(a) for a in axes)
    buffer, shapes = pack_rows(parts, count * 2)
    cell_count = micro_count * height * width * lax.axis_size("row") * lax.axis_size("col")
    grad_scale = 1.0 / math.sqrt(cell_count)
    loss_at = joined.shape[0] - 1

    def scale_of(position):
        return jnp.where(position == loss_at, 1.0 / cell_count, grad_scale).astype(jnp.float32)

    buffer, d_input = butterfly_psum(
        buffer, axes, [(3,), (6, 0), (1, 2), (4, 5)], scale_of, d_input, 2
    )
    joined, kernel_grad, expand_grad, project_grad, lateral_grad, classify_grad = unpack_rows(
        buffer, shapes
    )
    project_grad = project_grad.T
    sizes = [v.shape[0] for v in vectors]
    cuts = [sum(sizes[:k]) for k in range(len(sizes) + 1)]
    (
        convbias_grad,
        gain_grad,
        normbias_grad,
        expbias_grad,
        projbias_grad,
        layerscale_grad,
        latbias_grad,
        clsbias_grad,
        loss_total,
    ) = [joined[cuts[k] : cuts[k + 1]] for k in range(len(sizes))]
    return (
        d_input[None],
        loss_total[0],
        kernel_grad,
        convbias_grad,
        gain_grad,
        normbias_grad,
        expand_grad,
        expbias_grad,
        project_grad,
        projbias_grad,
        layerscale_grad,
        lateral_grad,
        latbias_grad,
        classify_grad,
        clsbias_grad,
    )


def solution(mesh):
    placed = (
        P(None, None, "row", "col"),
        P(None, "row", "col"),
        P(),
        P(),
        P(),
        P(),
        P(),
        P(),
        P(),
        P(),
        P(),
        P(),
        P(),
        P(),
        P(),
    )
    return jax.shard_map(
        shards,
        mesh=mesh,
        in_specs=placed,
        out_specs=(
            P("section", None, "row", "col"),
            P(),
            P(),
            P(),
            P(),
            P(),
            P(),
            P(),
            P(),
            P(),
            P(),
            P(),
            P(),
            P(),
            P(),
        ),
        check_vma=False,
    )
```

```python
import math

import jax
import jax.numpy as jnp
from jax import lax
from jax.sharding import PartitionSpec as P

EPSILON = 1e-06
ROOT_HALF = 0.7071067811865476
DENSITY_SCALE = 0.3989422804014327


def padded_2(x, sides, width):
    for axis, dim in sides:
        count, length = (lax.axis_size(axis), x.shape[dim])
        up = [(i, (i + 1) % count) for i in range(count - 1)]
        down = [(j, i) for i, j in up]
        order = (1, 0, 2) if dim == 1 else (2, 1, 0)
        last = jnp.transpose(lax.slice_in_dim(x, length - width, length, axis=dim), order)
        leading = jnp.transpose(lax.slice_in_dim(x, 0, width, axis=dim), order)
        before = jnp.transpose(lax.ppermute(last, axis, up), order)
        after = jnp.transpose(lax.ppermute(leading, axis, down), order)
        x = jnp.concatenate([before, x, after], axis=dim)
    return x


def from_behind(block, axis, distance):
    devices = range(lax.axis_size(axis))
    route = [(i - distance, i) for i in devices if i - distance in devices]
    return lax.ppermute(block, axis, route)


def product(form, left_side, right_side):
    return jnp.einsum(form, left_side, right_side, preferred_element_type=jnp.float32)


def depthwise(padded, kernel, height, width, flipped):
    total = jnp.zeros((padded.shape[0], height, width), jnp.float32)
    for tap_index in range(49):
        down_step = tap_index // 7
        side_step = tap_index % 7
        if flipped:
            down_step = 6 - down_step
            side_step = 6 - side_step
        window = padded[:, down_step : down_step + height, side_step : side_step + width].astype(
            jnp.float32
        )
        total = total + kernel[:, tap_index][:, None, None] * window
    return total


def normal_cdf(values):
    return 0.5 * (1.0 + lax.erf(values * ROOT_HALF))


def gelu_slope(values):
    return normal_cdf(values) + values * jnp.exp(-0.5 * values * values) * DENSITY_SCALE


def encoder_forward(padded, enc_params):
    dw_weight, dw_bias, norm_gain, norm_bias, w_in, b_in, w_out, b_out, layer_scale = enc_params
    height = padded.shape[1] - 6
    width = padded.shape[2] - 6
    conv = depthwise(padded, dw_weight, height, width, False) + dw_bias[:, None, None]
    centre = conv - jnp.mean(conv, axis=0, keepdims=True)
    inv_std = lax.rsqrt(jnp.mean(centre * centre, axis=0, keepdims=True) + EPSILON)
    scaled = centre * inv_std
    normed = (scaled * norm_gain[:, None, None] + norm_bias[:, None, None]).astype(jnp.bfloat16)
    before = product("chw,cd->dhw", normed, w_in) + b_in[:, None, None]
    active = (before * normal_cdf(before)).astype(jnp.bfloat16)
    branch = product("dhw,dc->chw", active, w_out) + b_out[:, None, None]
    inner = padded[:, 3 : 3 + height, 3 : 3 + width].astype(jnp.float32)
    output = (inner + layer_scale[:, None, None] * branch).astype(jnp.bfloat16)
    return (output, (scaled, inv_std, normed, before, active, branch))


def encoder_backward(saved, grad_out, enc_params):
    dw_weight, dw_bias, norm_gain, norm_bias, w_in, b_in, w_out, b_out, layer_scale = enc_params
    scaled, inv_std, normed, before, active, branch = saved
    grad_float = grad_out.astype(jnp.float32)
    layerscale_grad = jnp.sum(branch * grad_float, axis=(1, 2))
    d_branch = (layer_scale[:, None, None] * grad_float).astype(jnp.bfloat16)
    projbias_grad = jnp.sum(d_branch.astype(jnp.float32), axis=(1, 2))
    project_grad = product("dhw,chw->dc", active, d_branch)
    d_active = product("chw,dc->dhw", d_branch, w_out)
    d_before = (d_active * gelu_slope(before)).astype(jnp.bfloat16)
    expbias_grad = jnp.sum(d_before.astype(jnp.float32), axis=(1, 2))
    expand_grad = product("chw,dhw->cd", normed, d_before)
    d_normed = product("dhw,cd->chw", d_before, w_in)
    gain_grad = jnp.sum(d_normed * scaled, axis=(1, 2))
    normbias_grad = jnp.sum(d_normed, axis=(1, 2))
    d_scaled = d_normed * norm_gain[:, None, None]
    d_conv = inv_std * (
        d_scaled
        - jnp.mean(d_scaled, axis=0, keepdims=True)
        - scaled * jnp.mean(d_scaled * scaled, axis=0, keepdims=True)
    )
    grads = (
        gain_grad,
        normbias_grad,
        expand_grad,
        expbias_grad,
        project_grad,
        projbias_grad,
        layerscale_grad,
    )
    return (d_conv.astype(jnp.bfloat16), grads)


def conv_backward(padded, d_conv, d_padded, grad_out, dw_weight):
    height = d_conv.shape[1]
    width = d_conv.shape[2]
    d_input = grad_out.astype(jnp.float32) + depthwise(d_padded, dw_weight, height, width, True)
    conv_float = d_conv.astype(jnp.float32)
    columns = []
    for tap_index in range(49):
        down_step = tap_index // 7
        side_step = tap_index % 7
        window = padded[:, down_step : down_step + height, side_step : side_step + width].astype(
            jnp.float32
        )
        columns.append(jnp.sum(window * conv_float, axis=(1, 2)))
    kernel_grad = jnp.stack(columns, axis=1)
    convbias_grad = jnp.sum(conv_float, axis=(1, 2))
    return (d_input, kernel_grad, convbias_grad)


def decoder(encoded, label_tile, w_lateral, b_lateral, w_class, b_class):
    lateral_pre = product("chw,cl->lhw", encoded, w_lateral) + b_lateral[:, None, None]
    lateral = (lateral_pre * normal_cdf(lateral_pre)).astype(jnp.bfloat16)
    logits = product("lhw,lk->khw", lateral, w_class) + b_class[:, None, None]
    highest = jnp.max(logits, axis=0, keepdims=True)
    shifted = logits - highest
    totals = jnp.sum(jnp.exp(shifted), axis=0, keepdims=True)
    log_total = highest + jnp.log(totals)
    classes = jnp.arange(logits.shape[0], dtype=jnp.int32)
    onehot = (label_tile[None, :, :] == classes[:, None, None]).astype(jnp.float32)
    loss_sum = jnp.sum(log_total[0] - jnp.sum(onehot * logits, axis=0))
    d_logits = (jnp.exp(shifted) / totals - onehot).astype(jnp.bfloat16)
    classify_grad = product("lhw,khw->lk", lateral, d_logits)
    clsbias_grad = jnp.sum(d_logits.astype(jnp.float32), axis=(1, 2))
    d_lateral_raw = product("khw,lk->lhw", d_logits, w_class)
    d_lateral = (d_lateral_raw * gelu_slope(lateral_pre)).astype(jnp.bfloat16)
    lateral_grad = product("chw,lhw->cl", encoded, d_lateral)
    latbias_grad = jnp.sum(d_lateral.astype(jnp.float32), axis=(1, 2))
    d_encoded = product("lhw,cl->chw", d_lateral, w_lateral).astype(jnp.bfloat16)
    return (d_encoded, loss_sum, (lateral_grad, latbias_grad, classify_grad, clsbias_grad))


LANES = 128


def tile_order(x):
    rows, cols = x.shape
    x = x.reshape(rows // 8, 8, cols // LANES, LANES).transpose(0, 2, 1, 3)
    return x.reshape(rows * cols // LANES, LANES)


def from_tile_order(x, shape):
    rows, cols = shape
    x = x.reshape(rows // 8, cols // LANES, 8, LANES).transpose(0, 2, 1, 3)
    return x.reshape(rows, cols)


def tiled(shape):
    return len(shape) == 2 and shape[0] % 8 == 0 and shape[1] % LANES == 0


def pack_rows(parts, multiple):
    shapes, rows = [], []
    for part in parts:
        shapes.append(part.shape)
        if tiled(part.shape):
            rows.append(tile_order(part))
            continue
        flat = part.reshape(-1)
        size = flat.shape[0]
        padded_rows = -(-size // (8 * LANES)) * 8
        flat = jnp.pad(flat, (0, padded_rows * LANES - size))
        rows.append(flat.reshape(padded_rows, LANES))
    total = sum(r.shape[0] for r in rows)
    extra = -total % multiple
    if extra:
        rows.append(jnp.zeros((extra, LANES), jnp.float32))
    return jnp.concatenate(rows, axis=0), shapes


def unpack_rows(buffer, shapes):
    out, at = [], 0
    for shape in shapes:
        size = math.prod(shape)
        padded_rows = -(-size // (8 * LANES)) * 8
        piece = buffer[at : at + padded_rows]
        if tiled(shape):
            out.append(from_tile_order(piece, shape))
        else:
            out.append(piece.reshape(-1)[:size].reshape(shape))
        at += padded_rows
    return out


def spread(value, bits):
    out = 0
    for k, bit_at in enumerate(bits):
        if (value >> k) & 1:
            out |= 1 << bit_at
    return out


def butterfly_psum(buffer, axes, stages, scale_of, tie, tie_after):
    index = lax.axis_index(axes)
    count = math.prod(lax.axis_size(a) for a in axes)
    offset = jnp.zeros((), jnp.int32)
    places = []
    for bits in stages:
        ways = 1 << len(bits)
        mine = sum(((index >> bit_at) & 1) << k for k, bit_at in enumerate(bits))
        pieces = buffer.reshape(ways, buffer.shape[0] // ways, buffer.shape[1])
        total = lax.dynamic_index_in_dim(pieces, mine, 0, keepdims=False)
        for step in range(1, ways):
            flip = spread(step, bits)
            pairs = [(i, i ^ flip) for i in range(count)]
            send = lax.dynamic_index_in_dim(pieces, mine ^ step, 0, keepdims=False)
            total = total + lax.ppermute(send, axes, pairs)
        offset = offset * ways + mine
        places.append((bits, mine))
        buffer = total
        if len(places) == tie_after:
            buffer, tie = lax.optimization_barrier((buffer, tie))
    rows = buffer.shape[0]
    position = (offset * rows + lax.broadcasted_iota(jnp.int32, buffer.shape, 0)) * buffer.shape[1]
    position = position + lax.broadcasted_iota(jnp.int32, buffer.shape, 1)
    buffer = buffer * scale_of(position)
    for bits, mine in reversed(places):
        ways = 1 << len(bits)
        both = jnp.zeros((ways,) + buffer.shape, buffer.dtype)
        both = lax.dynamic_update_index_in_dim(both, buffer, mine, 0)
        for step in range(1, ways):
            flip = spread(step, bits)
            pairs = [(i, i ^ flip) for i in range(count)]
            other = lax.ppermute(buffer, axes, pairs)
            both = lax.dynamic_update_index_in_dim(both, other, mine ^ step, 0)
        buffer = both.reshape(-1, buffer.shape[1])
    return buffer, tie


def shards(
    features,
    labels,
    dw_weight,
    dw_bias,
    norm_gain,
    norm_bias,
    w_in,
    b_in,
    w_out,
    b_out,
    layer_scale,
    w_lateral,
    b_lateral,
    w_class,
    b_class,
):
    enc_params = (dw_weight, dw_bias, norm_gain, norm_bias, w_in, b_in, w_out, b_out, layer_scale)
    section = lax.axis_index("section")
    micro_count = features.shape[0]
    height = features.shape[2]
    width = features.shape[3]
    axes = ("section", "row", "col")

    def rimmed(tile):
        return padded_2(tile, (("row", 1), ("col", 2)), 3)

    tile = lax.dynamic_index_in_dim(features, section, 0, keepdims=False)
    label_tile = lax.dynamic_index_in_dim(labels, section, 0, keepdims=False)
    padded = rimmed(tile)
    output, saved = encoder_forward(padded, enc_params)
    returned, loss_sum, dec_grads = decoder(output, label_tile, w_lateral, b_lateral, w_class, b_class)
    d_conv, enc_grads = encoder_backward(saved, returned, enc_params)
    d_padded = rimmed(d_conv)
    d_input, kernel_grad, convbias_grad = conv_backward(padded, d_conv, d_padded, returned, dw_weight)
    (
        gain_grad,
        normbias_grad,
        expand_grad,
        expbias_grad,
        project_grad,
        projbias_grad,
        layerscale_grad,
    ) = enc_grads
    lateral_grad, latbias_grad, classify_grad, clsbias_grad = dec_grads
    vectors = [convbias_grad, gain_grad, normbias_grad, expbias_grad, projbias_grad]
    vectors += [layerscale_grad, latbias_grad, clsbias_grad, loss_sum.reshape(1)]
    joined = jnp.concatenate(vectors)
    parts = [joined, kernel_grad, expand_grad, project_grad.T, lateral_grad, classify_grad]
    count = math.prod(lax.axis_size(a) for a in axes)
    buffer, shapes = pack_rows(parts, count * 2)
    cell_count = micro_count * height * width * lax.axis_size("row") * lax.axis_size("col")
    grad_scale = 1.0 / math.sqrt(cell_count)
    loss_at = joined.shape[0] - 1

    def scale_of(position):
        return jnp.where(position == loss_at, 1.0 / cell_count, grad_scale).astype(jnp.float32)

    buffer, d_input = butterfly_psum(
        buffer, axes, [(3,), (6, 0), (1, 2, 4, 5)], scale_of, d_input, 2
    )
    joined, kernel_grad, expand_grad, project_grad, lateral_grad, classify_grad = unpack_rows(
        buffer, shapes
    )
    project_grad = project_grad.T
    sizes = [v.shape[0] for v in vectors]
    cuts = [sum(sizes[:k]) for k in range(len(sizes) + 1)]
    (
        convbias_grad,
        gain_grad,
        normbias_grad,
        expbias_grad,
        projbias_grad,
        layerscale_grad,
        latbias_grad,
        clsbias_grad,
        loss_total,
    ) = [joined[cuts[k] : cuts[k + 1]] for k in range(len(sizes))]
    return (
        d_input[None],
        loss_total[0],
        kernel_grad,
        convbias_grad,
        gain_grad,
        normbias_grad,
        expand_grad,
        expbias_grad,
        project_grad,
        projbias_grad,
        layerscale_grad,
        lateral_grad,
        latbias_grad,
        classify_grad,
        clsbias_grad,
    )


def solution(mesh):
    placed = (
        P(None, None, "row", "col"),
        P(None, "row", "col"),
        P(),
        P(),
        P(),
        P(),
        P(),
        P(),
        P(),
        P(),
        P(),
        P(),
        P(),
        P(),
        P(),
    )
    return jax.shard_map(
        shards,
        mesh=mesh,
        in_specs=placed,
        out_specs=(
            P("section", None, "row", "col"),
            P(),
            P(),
            P(),
            P(),
            P(),
            P(),
            P(),
            P(),
            P(),
            P(),
            P(),
            P(),
            P(),
            P(),
        ),
        check_vma=False,
    )
```

```python
import math

import jax
import jax.numpy as jnp
from jax import lax
from jax.sharding import PartitionSpec as P

EPSILON = 1e-06
ROOT_HALF = 0.7071067811865476
DENSITY_SCALE = 0.3989422804014327


def padded_2(x, sides, width):
    for axis, dim in sides:
        count, length = (lax.axis_size(axis), x.shape[dim])
        up = [(i, (i + 1) % count) for i in range(count - 1)]
        down = [(j, i) for i, j in up]
        order = (1, 0, 2) if dim == 1 else (2, 1, 0)
        last = jnp.transpose(lax.slice_in_dim(x, length - width, length, axis=dim), order)
        leading = jnp.transpose(lax.slice_in_dim(x, 0, width, axis=dim), order)
        before = jnp.transpose(lax.ppermute(last, axis, up), order)
        after = jnp.transpose(lax.ppermute(leading, axis, down), order)
        x = jnp.concatenate([before, x, after], axis=dim)
    return x


def from_behind(block, axis, distance):
    devices = range(lax.axis_size(axis))
    route = [(i - distance, i) for i in devices if i - distance in devices]
    return lax.ppermute(block, axis, route)


def product(form, left_side, right_side):
    return jnp.einsum(form, left_side, right_side, preferred_element_type=jnp.float32)


def depthwise(padded, kernel, height, width, flipped):
    total = jnp.zeros((padded.shape[0], height, width), jnp.float32)
    for tap_index in range(49):
        down_step = tap_index // 7
        side_step = tap_index % 7
        if flipped:
            down_step = 6 - down_step
            side_step = 6 - side_step
        window = padded[:, down_step : down_step + height, side_step : side_step + width].astype(
            jnp.float32
        )
        total = total + kernel[:, tap_index][:, None, None] * window
    return total


def normal_cdf(values):
    return 0.5 * (1.0 + lax.erf(values * ROOT_HALF))


def gelu_slope(values):
    return normal_cdf(values) + values * jnp.exp(-0.5 * values * values) * DENSITY_SCALE


def encoder_forward(padded, enc_params):
    dw_weight, dw_bias, norm_gain, norm_bias, w_in, b_in, w_out, b_out, layer_scale = enc_params
    height = padded.shape[1] - 6
    width = padded.shape[2] - 6
    conv = depthwise(padded, dw_weight, height, width, False) + dw_bias[:, None, None]
    centre = conv - jnp.mean(conv, axis=0, keepdims=True)
    inv_std = lax.rsqrt(jnp.mean(centre * centre, axis=0, keepdims=True) + EPSILON)
    scaled = centre * inv_std
    normed = (scaled * norm_gain[:, None, None] + norm_bias[:, None, None]).astype(jnp.bfloat16)
    before = product("chw,cd->dhw", normed, w_in) + b_in[:, None, None]
    active = (before * normal_cdf(before)).astype(jnp.bfloat16)
    branch = product("dhw,dc->chw", active, w_out) + b_out[:, None, None]
    inner = padded[:, 3 : 3 + height, 3 : 3 + width].astype(jnp.float32)
    output = (inner + layer_scale[:, None, None] * branch).astype(jnp.bfloat16)
    return (output, (scaled, inv_std, normed, before, active, branch))


def encoder_backward(saved, grad_out, enc_params):
    dw_weight, dw_bias, norm_gain, norm_bias, w_in, b_in, w_out, b_out, layer_scale = enc_params
    scaled, inv_std, normed, before, active, branch = saved
    grad_float = grad_out.astype(jnp.float32)
    layerscale_grad = jnp.sum(branch * grad_float, axis=(1, 2))
    d_branch = (layer_scale[:, None, None] * grad_float).astype(jnp.bfloat16)
    projbias_grad = jnp.sum(d_branch.astype(jnp.float32), axis=(1, 2))
    project_grad = product("dhw,chw->dc", active, d_branch)
    d_active = product("chw,dc->dhw", d_branch, w_out)
    d_before = (d_active * gelu_slope(before)).astype(jnp.bfloat16)
    expbias_grad = jnp.sum(d_before.astype(jnp.float32), axis=(1, 2))
    expand_grad = product("chw,dhw->cd", normed, d_before)
    d_normed = product("dhw,cd->chw", d_before, w_in)
    gain_grad = jnp.sum(d_normed * scaled, axis=(1, 2))
    normbias_grad = jnp.sum(d_normed, axis=(1, 2))
    d_scaled = d_normed * norm_gain[:, None, None]
    d_conv = inv_std * (
        d_scaled
        - jnp.mean(d_scaled, axis=0, keepdims=True)
        - scaled * jnp.mean(d_scaled * scaled, axis=0, keepdims=True)
    )
    grads = (
        gain_grad,
        normbias_grad,
        expand_grad,
        expbias_grad,
        project_grad,
        projbias_grad,
        layerscale_grad,
    )
    return (d_conv.astype(jnp.bfloat16), grads)


def conv_backward(padded, d_conv, d_padded, grad_out, dw_weight):
    height = d_conv.shape[1]
    width = d_conv.shape[2]
    d_input = grad_out.astype(jnp.float32) + depthwise(d_padded, dw_weight, height, width, True)
    conv_float = d_conv.astype(jnp.float32)
    columns = []
    for tap_index in range(49):
        down_step = tap_index // 7
        side_step = tap_index % 7
        window = padded[:, down_step : down_step + height, side_step : side_step + width].astype(
            jnp.float32
        )
        columns.append(jnp.sum(window * conv_float, axis=(1, 2)))
    kernel_grad = jnp.stack(columns, axis=1)
    convbias_grad = jnp.sum(conv_float, axis=(1, 2))
    return (d_input, kernel_grad, convbias_grad)


def decoder(encoded, label_tile, w_lateral, b_lateral, w_class, b_class):
    lateral_pre = product("chw,cl->lhw", encoded, w_lateral) + b_lateral[:, None, None]
    lateral = (lateral_pre * normal_cdf(lateral_pre)).astype(jnp.bfloat16)
    logits = product("lhw,lk->khw", lateral, w_class) + b_class[:, None, None]
    highest = jnp.max(logits, axis=0, keepdims=True)
    shifted = logits - highest
    totals = jnp.sum(jnp.exp(shifted), axis=0, keepdims=True)
    log_total = highest + jnp.log(totals)
    classes = jnp.arange(logits.shape[0], dtype=jnp.int32)
    onehot = (label_tile[None, :, :] == classes[:, None, None]).astype(jnp.float32)
    loss_sum = jnp.sum(log_total[0] - jnp.sum(onehot * logits, axis=0))
    d_logits = (jnp.exp(shifted) / totals - onehot).astype(jnp.bfloat16)
    classify_grad = product("lhw,khw->lk", lateral, d_logits)
    clsbias_grad = jnp.sum(d_logits.astype(jnp.float32), axis=(1, 2))
    d_lateral_raw = product("khw,lk->lhw", d_logits, w_class)
    d_lateral = (d_lateral_raw * gelu_slope(lateral_pre)).astype(jnp.bfloat16)
    lateral_grad = product("chw,lhw->cl", encoded, d_lateral)
    latbias_grad = jnp.sum(d_lateral.astype(jnp.float32), axis=(1, 2))
    d_encoded = product("lhw,cl->chw", d_lateral, w_lateral).astype(jnp.bfloat16)
    return (d_encoded, loss_sum, (lateral_grad, latbias_grad, classify_grad, clsbias_grad))


LANES = 128


def tile_order(x):
    rows, cols = x.shape
    x = x.reshape(rows // 8, 8, cols // LANES, LANES).transpose(0, 2, 1, 3)
    return x.reshape(rows * cols // LANES, LANES)


def from_tile_order(x, shape):
    rows, cols = shape
    x = x.reshape(rows // 8, cols // LANES, 8, LANES).transpose(0, 2, 1, 3)
    return x.reshape(rows, cols)


def tiled(shape):
    return len(shape) == 2 and shape[0] % 8 == 0 and shape[1] % LANES == 0


def pack_rows(parts, multiple):
    shapes, rows = [], []
    for part in parts:
        shapes.append(part.shape)
        if tiled(part.shape):
            rows.append(tile_order(part))
            continue
        flat = part.reshape(-1)
        size = flat.shape[0]
        padded_rows = -(-size // (8 * LANES)) * 8
        flat = jnp.pad(flat, (0, padded_rows * LANES - size))
        rows.append(flat.reshape(padded_rows, LANES))
    total = sum(r.shape[0] for r in rows)
    extra = -total % multiple
    if extra:
        rows.append(jnp.zeros((extra, LANES), jnp.float32))
    return jnp.concatenate(rows, axis=0), shapes


def unpack_rows(buffer, shapes):
    out, at = [], 0
    for shape in shapes:
        size = math.prod(shape)
        padded_rows = -(-size // (8 * LANES)) * 8
        piece = buffer[at : at + padded_rows]
        if tiled(shape):
            out.append(from_tile_order(piece, shape))
        else:
            out.append(piece.reshape(-1)[:size].reshape(shape))
        at += padded_rows
    return out


def spread(value, bits):
    out = 0
    for k, bit_at in enumerate(bits):
        if (value >> k) & 1:
            out |= 1 << bit_at
    return out


def butterfly_psum(buffer, axes, stages, scale_of, ties):
    index = lax.axis_index(axes)
    count = math.prod(lax.axis_size(a) for a in axes)
    offset = jnp.zeros((), jnp.int32)
    places = []
    for bits in stages:
        ways = 1 << len(bits)
        mine = sum(((index >> bit_at) & 1) << k for k, bit_at in enumerate(bits))
        pieces = buffer.reshape(ways, buffer.shape[0] // ways, buffer.shape[1])
        total = lax.dynamic_index_in_dim(pieces, mine, 0, keepdims=False)
        for step in range(1, ways):
            flip = spread(step, bits)
            pairs = [(i, i ^ flip) for i in range(count)]
            send = lax.dynamic_index_in_dim(pieces, mine ^ step, 0, keepdims=False)
            total = total + lax.ppermute(send, axes, pairs)
        offset = offset * ways + mine
        places.append((bits, mine))
        buffer = total
        if len(places) in ties:
            buffer, ties[len(places)] = lax.optimization_barrier((buffer, ties[len(places)]))
    rows = buffer.shape[0]
    position = (offset * rows + lax.broadcasted_iota(jnp.int32, buffer.shape, 0)) * buffer.shape[1]
    position = position + lax.broadcasted_iota(jnp.int32, buffer.shape, 1)
    buffer = buffer * scale_of(position)
    for bits, mine in reversed(places):
        ways = 1 << len(bits)
        both = jnp.zeros((ways,) + buffer.shape, buffer.dtype)
        both = lax.dynamic_update_index_in_dim(both, buffer, mine, 0)
        for step in range(1, ways):
            flip = spread(step, bits)
            pairs = [(i, i ^ flip) for i in range(count)]
            other = lax.ppermute(buffer, axes, pairs)
            both = lax.dynamic_update_index_in_dim(both, other, mine ^ step, 0)
        buffer = both.reshape(-1, buffer.shape[1])
    return buffer, ties


def shards(
    features,
    labels,
    dw_weight,
    dw_bias,
    norm_gain,
    norm_bias,
    w_in,
    b_in,
    w_out,
    b_out,
    layer_scale,
    w_lateral,
    b_lateral,
    w_class,
    b_class,
):
    enc_params = (dw_weight, dw_bias, norm_gain, norm_bias, w_in, b_in, w_out, b_out, layer_scale)
    section = lax.axis_index("section")
    micro_count = features.shape[0]
    height = features.shape[2]
    width = features.shape[3]
    axes = ("section", "row", "col")

    def rimmed(tile):
        return padded_2(tile, (("row", 1), ("col", 2)), 3)

    tile = lax.dynamic_index_in_dim(features, section, 0, keepdims=False)
    label_tile = lax.dynamic_index_in_dim(labels, section, 0, keepdims=False)
    padded = rimmed(tile)
    output, saved = encoder_forward(padded, enc_params)
    returned, loss_sum, dec_grads = decoder(output, label_tile, w_lateral, b_lateral, w_class, b_class)
    d_conv, enc_grads = encoder_backward(saved, returned, enc_params)
    d_padded = rimmed(d_conv)
    d_input, kernel_grad, convbias_grad = conv_backward(padded, d_conv, d_padded, returned, dw_weight)
    (
        gain_grad,
        normbias_grad,
        expand_grad,
        expbias_grad,
        project_grad,
        projbias_grad,
        layerscale_grad,
    ) = enc_grads
    lateral_grad, latbias_grad, classify_grad, clsbias_grad = dec_grads
    vectors = [convbias_grad, gain_grad, normbias_grad, expbias_grad, projbias_grad]
    vectors += [layerscale_grad, latbias_grad, clsbias_grad, loss_sum.reshape(1)]
    joined = jnp.concatenate(vectors)
    parts = [joined, kernel_grad, expand_grad, project_grad.T, lateral_grad, classify_grad]
    count = math.prod(lax.axis_size(a) for a in axes)
    buffer, shapes = pack_rows(parts, count * 2)
    cell_count = micro_count * height * width * lax.axis_size("row") * lax.axis_size("col")
    grad_scale = 1.0 / math.sqrt(cell_count)
    loss_at = joined.shape[0] - 1

    def scale_of(position):
        return jnp.where(position == loss_at, 1.0 / cell_count, grad_scale).astype(jnp.float32)

    half = d_conv.shape[0] // 2

    def input_part(low, high):
        flipped = depthwise(d_padded[low:high], dw_weight[low:high], height, width, True)
        return returned[low:high].astype(jnp.float32) + flipped

    ties = {2: input_part(0, half), 3: input_part(half, d_conv.shape[0])}
    buffer, ties = butterfly_psum(buffer, axes, [(3,), (6, 0), (1, 2), (4, 5)], scale_of, ties)
    d_input = jnp.concatenate([ties[2], ties[3]], axis=0)
    joined, kernel_grad, expand_grad, project_grad, lateral_grad, classify_grad = unpack_rows(
        buffer, shapes
    )
    project_grad = project_grad.T
    sizes = [v.shape[0] for v in vectors]
    cuts = [sum(sizes[:k]) for k in range(len(sizes) + 1)]
    (
        convbias_grad,
        gain_grad,
        normbias_grad,
        expbias_grad,
        projbias_grad,
        layerscale_grad,
        latbias_grad,
        clsbias_grad,
        loss_total,
    ) = [joined[cuts[k] : cuts[k + 1]] for k in range(len(sizes))]
    return (
        d_input[None],
        loss_total[0],
        kernel_grad,
        convbias_grad,
        gain_grad,
        normbias_grad,
        expand_grad,
        expbias_grad,
        project_grad,
        projbias_grad,
        layerscale_grad,
        lateral_grad,
        latbias_grad,
        classify_grad,
        clsbias_grad,
    )


def solution(mesh):
    placed = (
        P(None, None, "row", "col"),
        P(None, "row", "col"),
        P(),
        P(),
        P(),
        P(),
        P(),
        P(),
        P(),
        P(),
        P(),
        P(),
        P(),
        P(),
        P(),
    )
    return jax.shard_map(
        shards,
        mesh=mesh,
        in_specs=placed,
        out_specs=(
            P("section", None, "row", "col"),
            P(),
            P(),
            P(),
            P(),
            P(),
            P(),
            P(),
            P(),
            P(),
            P(),
            P(),
            P(),
            P(),
            P(),
        ),
        check_vma=False,
    )
```

```python
import math

import jax
import jax.numpy as jnp
from jax import lax
from jax.sharding import PartitionSpec as P

EPSILON = 1e-06
ROOT_HALF = 0.7071067811865476
DENSITY_SCALE = 0.3989422804014327


def padded_2(x, sides, width):
    for axis, dim in sides:
        count, length = (lax.axis_size(axis), x.shape[dim])
        up = [(i, (i + 1) % count) for i in range(count - 1)]
        down = [(j, i) for i, j in up]
        order = (1, 0, 2) if dim == 1 else (2, 1, 0)
        last = jnp.transpose(lax.slice_in_dim(x, length - width, length, axis=dim), order)
        leading = jnp.transpose(lax.slice_in_dim(x, 0, width, axis=dim), order)
        before = jnp.transpose(lax.ppermute(last, axis, up), order)
        after = jnp.transpose(lax.ppermute(leading, axis, down), order)
        x = jnp.concatenate([before, x, after], axis=dim)
    return x


def from_behind(block, axis, distance):
    devices = range(lax.axis_size(axis))
    route = [(i - distance, i) for i in devices if i - distance in devices]
    return lax.ppermute(block, axis, route)


def product(form, left_side, right_side):
    return jnp.einsum(form, left_side, right_side, preferred_element_type=jnp.float32)


def depthwise(padded, kernel, height, width, flipped):
    total = jnp.zeros((padded.shape[0], height, width), jnp.float32)
    for tap_index in range(49):
        down_step = tap_index // 7
        side_step = tap_index % 7
        if flipped:
            down_step = 6 - down_step
            side_step = 6 - side_step
        window = padded[:, down_step : down_step + height, side_step : side_step + width].astype(
            jnp.float32
        )
        total = total + kernel[:, tap_index][:, None, None] * window
    return total


def normal_cdf(values):
    return 0.5 * (1.0 + lax.erf(values * ROOT_HALF))


def gelu_slope(values):
    return normal_cdf(values) + values * jnp.exp(-0.5 * values * values) * DENSITY_SCALE


def encoder_forward(padded, enc_params):
    dw_weight, dw_bias, norm_gain, norm_bias, w_in, b_in, w_out, b_out, layer_scale = enc_params
    height = padded.shape[1] - 6
    width = padded.shape[2] - 6
    conv = depthwise(padded, dw_weight, height, width, False) + dw_bias[:, None, None]
    centre = conv - jnp.mean(conv, axis=0, keepdims=True)
    inv_std = lax.rsqrt(jnp.mean(centre * centre, axis=0, keepdims=True) + EPSILON)
    scaled = centre * inv_std
    normed = (scaled * norm_gain[:, None, None] + norm_bias[:, None, None]).astype(jnp.bfloat16)
    before = product("chw,cd->dhw", normed, w_in) + b_in[:, None, None]
    active = (before * normal_cdf(before)).astype(jnp.bfloat16)
    branch = product("dhw,dc->chw", active, w_out) + b_out[:, None, None]
    inner = padded[:, 3 : 3 + height, 3 : 3 + width].astype(jnp.float32)
    output = (inner + layer_scale[:, None, None] * branch).astype(jnp.bfloat16)
    return (output, (scaled, inv_std, normed, before, active, branch))


def encoder_backward(saved, grad_out, enc_params):
    dw_weight, dw_bias, norm_gain, norm_bias, w_in, b_in, w_out, b_out, layer_scale = enc_params
    scaled, inv_std, normed, before, active, branch = saved
    grad_float = grad_out.astype(jnp.float32)
    layerscale_grad = jnp.sum(branch * grad_float, axis=(1, 2))
    d_branch = (layer_scale[:, None, None] * grad_float).astype(jnp.bfloat16)
    projbias_grad = jnp.sum(d_branch.astype(jnp.float32), axis=(1, 2))
    project_grad = product("dhw,chw->dc", active, d_branch)
    d_active = product("chw,dc->dhw", d_branch, w_out)
    d_before = (d_active * gelu_slope(before)).astype(jnp.bfloat16)
    expbias_grad = jnp.sum(d_before.astype(jnp.float32), axis=(1, 2))
    expand_grad = product("chw,dhw->cd", normed, d_before)
    d_normed = product("dhw,cd->chw", d_before, w_in)
    gain_grad = jnp.sum(d_normed * scaled, axis=(1, 2))
    normbias_grad = jnp.sum(d_normed, axis=(1, 2))
    d_scaled = d_normed * norm_gain[:, None, None]
    d_conv = inv_std * (
        d_scaled
        - jnp.mean(d_scaled, axis=0, keepdims=True)
        - scaled * jnp.mean(d_scaled * scaled, axis=0, keepdims=True)
    )
    grads = (
        gain_grad,
        normbias_grad,
        expand_grad,
        expbias_grad,
        project_grad,
        projbias_grad,
        layerscale_grad,
    )
    return (d_conv.astype(jnp.bfloat16), grads)


def conv_backward(padded, d_conv, d_padded, grad_out, dw_weight):
    height = d_conv.shape[1]
    width = d_conv.shape[2]
    d_input = grad_out.astype(jnp.float32) + depthwise(d_padded, dw_weight, height, width, True)
    conv_float = d_conv.astype(jnp.float32)
    columns = []
    for tap_index in range(49):
        down_step = tap_index // 7
        side_step = tap_index % 7
        window = padded[:, down_step : down_step + height, side_step : side_step + width].astype(
            jnp.float32
        )
        columns.append(jnp.sum(window * conv_float, axis=(1, 2)))
    kernel_grad = jnp.stack(columns, axis=1)
    convbias_grad = jnp.sum(conv_float, axis=(1, 2))
    return (d_input, kernel_grad, convbias_grad)


def decoder(encoded, label_tile, w_lateral, b_lateral, w_class, b_class):
    lateral_pre = product("chw,cl->lhw", encoded, w_lateral) + b_lateral[:, None, None]
    lateral = (lateral_pre * normal_cdf(lateral_pre)).astype(jnp.bfloat16)
    logits = product("lhw,lk->khw", lateral, w_class) + b_class[:, None, None]
    highest = jnp.max(logits, axis=0, keepdims=True)
    shifted = logits - highest
    totals = jnp.sum(jnp.exp(shifted), axis=0, keepdims=True)
    log_total = highest + jnp.log(totals)
    classes = jnp.arange(logits.shape[0], dtype=jnp.int32)
    onehot = (label_tile[None, :, :] == classes[:, None, None]).astype(jnp.float32)
    loss_sum = jnp.sum(log_total[0] - jnp.sum(onehot * logits, axis=0))
    d_logits = (jnp.exp(shifted) / totals - onehot).astype(jnp.bfloat16)
    classify_grad = product("lhw,khw->lk", lateral, d_logits)
    clsbias_grad = jnp.sum(d_logits.astype(jnp.float32), axis=(1, 2))
    d_lateral_raw = product("khw,lk->lhw", d_logits, w_class)
    d_lateral = (d_lateral_raw * gelu_slope(lateral_pre)).astype(jnp.bfloat16)
    lateral_grad = product("chw,lhw->cl", encoded, d_lateral)
    latbias_grad = jnp.sum(d_lateral.astype(jnp.float32), axis=(1, 2))
    d_encoded = product("lhw,cl->chw", d_lateral, w_lateral).astype(jnp.bfloat16)
    return (d_encoded, loss_sum, (lateral_grad, latbias_grad, classify_grad, clsbias_grad))


LANES = 128


def tile_order(x):
    rows, cols = x.shape
    x = x.reshape(rows // 8, 8, cols // LANES, LANES).transpose(0, 2, 1, 3)
    return x.reshape(rows * cols // LANES, LANES)


def from_tile_order(x, shape):
    rows, cols = shape
    x = x.reshape(rows // 8, cols // LANES, 8, LANES).transpose(0, 2, 1, 3)
    return x.reshape(rows, cols)


def tiled(shape):
    return len(shape) == 2 and shape[0] % 8 == 0 and shape[1] % LANES == 0


def pack_rows(parts, multiple):
    shapes, rows = [], []
    for part in parts:
        shapes.append(part.shape)
        if tiled(part.shape):
            rows.append(tile_order(part))
            continue
        flat = part.reshape(-1)
        size = flat.shape[0]
        padded_rows = -(-size // (8 * LANES)) * 8
        flat = jnp.pad(flat, (0, padded_rows * LANES - size))
        rows.append(flat.reshape(padded_rows, LANES))
    total = sum(r.shape[0] for r in rows)
    extra = -total % multiple
    if extra:
        rows.append(jnp.zeros((extra, LANES), jnp.float32))
    return jnp.concatenate(rows, axis=0), shapes


def pack_rotated(parts, multiple, turn):
    blocks, shapes = [], []
    for part in parts:
        shapes.append(part.shape)
        if tiled(part.shape):
            blocks.append(tile_order(part))
            continue
        flat = part.reshape(-1)
        size = flat.shape[0]
        padded_rows = -(-size // (8 * LANES)) * 8
        blocks.append(jnp.pad(flat, (0, padded_rows * LANES - size)).reshape(padded_rows, LANES))
    total = sum(b.shape[0] for b in blocks)
    total += -total % multiple
    half = total // 2
    buffer = jnp.zeros((total, LANES), jnp.float32)
    at = 0
    for block in blocks:
        pieces = [(block, at)]
        if at < half < at + block.shape[0]:
            pieces = [(block[: half - at], at), (block[half - at :], half)]
        for piece, start in pieces:
            place = (start + turn * half) % total
            buffer = lax.dynamic_update_slice_in_dim(buffer, piece, place, 0)
        at += block.shape[0]
    return buffer, shapes


def unpack_rows(buffer, shapes):
    out, at = [], 0
    for shape in shapes:
        size = math.prod(shape)
        padded_rows = -(-size // (8 * LANES)) * 8
        piece = buffer[at : at + padded_rows]
        if tiled(shape):
            out.append(from_tile_order(piece, shape))
        else:
            out.append(piece.reshape(-1)[:size].reshape(shape))
        at += padded_rows
    return out


def spread(value, bits):
    out = 0
    for k, bit_at in enumerate(bits):
        if (value >> k) & 1:
            out |= 1 << bit_at
    return out


def butterfly_psum(buffer, axes, stages, scale_of, ties):
    index = lax.axis_index(axes)
    count = math.prod(lax.axis_size(a) for a in axes)
    offset = jnp.zeros((), jnp.int32)
    places = []
    for bits in stages:
        ways = 1 << len(bits)
        mine = sum(((index >> bit_at) & 1) << k for k, bit_at in enumerate(bits))
        pieces = buffer.reshape(ways, buffer.shape[0] // ways, buffer.shape[1])
        turned = not places
        total = pieces[0] if turned else lax.dynamic_index_in_dim(pieces, mine, 0, keepdims=False)
        for step in range(1, ways):
            flip = spread(step, bits)
            pairs = [(i, i ^ flip) for i in range(count)]
            if turned:
                send = pieces[step]
            else:
                send = lax.dynamic_index_in_dim(pieces, mine ^ step, 0, keepdims=False)
            total = total + lax.ppermute(send, axes, pairs)
        offset = offset * ways + mine
        places.append((bits, mine))
        buffer = total
        if len(places) in ties:
            buffer, ties[len(places)] = lax.optimization_barrier((buffer, ties[len(places)]))
    rows = buffer.shape[0]
    position = (offset * rows + lax.broadcasted_iota(jnp.int32, buffer.shape, 0)) * buffer.shape[1]
    position = position + lax.broadcasted_iota(jnp.int32, buffer.shape, 1)
    buffer = buffer * scale_of(position)
    for bits, mine in reversed(places):
        ways = 1 << len(bits)
        both = jnp.zeros((ways,) + buffer.shape, buffer.dtype)
        both = lax.dynamic_update_index_in_dim(both, buffer, mine, 0)
        for step in range(1, ways):
            flip = spread(step, bits)
            pairs = [(i, i ^ flip) for i in range(count)]
            other = lax.ppermute(buffer, axes, pairs)
            both = lax.dynamic_update_index_in_dim(both, other, mine ^ step, 0)
        buffer = both.reshape(-1, buffer.shape[1])
    return buffer, ties


def shards(
    features,
    labels,
    dw_weight,
    dw_bias,
    norm_gain,
    norm_bias,
    w_in,
    b_in,
    w_out,
    b_out,
    layer_scale,
    w_lateral,
    b_lateral,
    w_class,
    b_class,
):
    enc_params = (dw_weight, dw_bias, norm_gain, norm_bias, w_in, b_in, w_out, b_out, layer_scale)
    section = lax.axis_index("section")
    micro_count = features.shape[0]
    height = features.shape[2]
    width = features.shape[3]
    axes = ("section", "row", "col")

    def rimmed(tile):
        return padded_2(tile, (("row", 1), ("col", 2)), 3)

    tile = lax.dynamic_index_in_dim(features, section, 0, keepdims=False)
    label_tile = lax.dynamic_index_in_dim(labels, section, 0, keepdims=False)
    padded = rimmed(tile)
    output, saved = encoder_forward(padded, enc_params)
    returned, loss_sum, dec_grads = decoder(output, label_tile, w_lateral, b_lateral, w_class, b_class)
    d_conv, enc_grads = encoder_backward(saved, returned, enc_params)
    d_padded = rimmed(d_conv)
    d_input, kernel_grad, convbias_grad = conv_backward(padded, d_conv, d_padded, returned, dw_weight)
    (
        gain_grad,
        normbias_grad,
        expand_grad,
        expbias_grad,
        project_grad,
        projbias_grad,
        layerscale_grad,
    ) = enc_grads
    lateral_grad, latbias_grad, classify_grad, clsbias_grad = dec_grads
    vectors = [convbias_grad, gain_grad, normbias_grad, expbias_grad, projbias_grad]
    vectors += [layerscale_grad, latbias_grad, clsbias_grad, loss_sum.reshape(1)]
    joined = jnp.concatenate(vectors)
    parts = [joined, kernel_grad, expand_grad, project_grad.T, lateral_grad, classify_grad]
    count = math.prod(lax.axis_size(a) for a in axes)
    turn = (lax.axis_index(axes) >> 3) & 1
    buffer, shapes = pack_rotated(parts, count * 2, turn)
    cell_count = micro_count * height * width * lax.axis_size("row") * lax.axis_size("col")
    grad_scale = 1.0 / math.sqrt(cell_count)
    loss_at = joined.shape[0] - 1

    def scale_of(position):
        return jnp.where(position == loss_at, 1.0 / cell_count, grad_scale).astype(jnp.float32)

    half = d_conv.shape[0] // 2

    def input_part(low, high):
        flipped = depthwise(d_padded[low:high], dw_weight[low:high], height, width, True)
        return returned[low:high].astype(jnp.float32) + flipped

    ties = {2: input_part(0, half), 3: input_part(half, d_conv.shape[0])}
    buffer, ties = butterfly_psum(buffer, axes, [(3,), (6, 0), (1, 2), (4, 5)], scale_of, ties)
    d_input = jnp.concatenate([ties[2], ties[3]], axis=0)
    joined, kernel_grad, expand_grad, project_grad, lateral_grad, classify_grad = unpack_rows(
        buffer, shapes
    )
    project_grad = project_grad.T
    sizes = [v.shape[0] for v in vectors]
    cuts = [sum(sizes[:k]) for k in range(len(sizes) + 1)]
    (
        convbias_grad,
        gain_grad,
        normbias_grad,
        expbias_grad,
        projbias_grad,
        layerscale_grad,
        latbias_grad,
        clsbias_grad,
        loss_total,
    ) = [joined[cuts[k] : cuts[k + 1]] for k in range(len(sizes))]
    return (
        d_input[None],
        loss_total[0],
        kernel_grad,
        convbias_grad,
        gain_grad,
        normbias_grad,
        expand_grad,
        expbias_grad,
        project_grad,
        projbias_grad,
        layerscale_grad,
        lateral_grad,
        latbias_grad,
        classify_grad,
        clsbias_grad,
    )


def solution(mesh):
    placed = (
        P(None, None, "row", "col"),
        P(None, "row", "col"),
        P(),
        P(),
        P(),
        P(),
        P(),
        P(),
        P(),
        P(),
        P(),
        P(),
        P(),
        P(),
        P(),
    )
    return jax.shard_map(
        shards,
        mesh=mesh,
        in_specs=placed,
        out_specs=(
            P("section", None, "row", "col"),
            P(),
            P(),
            P(),
            P(),
            P(),
            P(),
            P(),
            P(),
            P(),
            P(),
            P(),
            P(),
            P(),
            P(),
        ),
        check_vma=False,
    )
```

```python
import math

import jax
import jax.numpy as jnp
from jax import lax
from jax.sharding import PartitionSpec as P

EPSILON = 1e-06
ROOT_HALF = 0.7071067811865476
DENSITY_SCALE = 0.3989422804014327


def padded_2(x, sides, width):
    for axis, dim in sides:
        count, length = (lax.axis_size(axis), x.shape[dim])
        up = [(i, (i + 1) % count) for i in range(count - 1)]
        down = [(j, i) for i, j in up]
        order = (1, 0, 2) if dim == 1 else (2, 1, 0)
        last = jnp.transpose(lax.slice_in_dim(x, length - width, length, axis=dim), order)
        leading = jnp.transpose(lax.slice_in_dim(x, 0, width, axis=dim), order)
        before = jnp.transpose(lax.ppermute(last, axis, up), order)
        after = jnp.transpose(lax.ppermute(leading, axis, down), order)
        x = jnp.concatenate([before, x, after], axis=dim)
    return x


def from_behind(block, axis, distance):
    devices = range(lax.axis_size(axis))
    route = [(i - distance, i) for i in devices if i - distance in devices]
    return lax.ppermute(block, axis, route)


def product(form, left_side, right_side):
    return jnp.einsum(form, left_side, right_side, preferred_element_type=jnp.float32)


def depthwise(padded, kernel, height, width, flipped):
    total = jnp.zeros((padded.shape[0], height, width), jnp.float32)
    for tap_index in range(49):
        down_step = tap_index // 7
        side_step = tap_index % 7
        if flipped:
            down_step = 6 - down_step
            side_step = 6 - side_step
        window = padded[:, down_step : down_step + height, side_step : side_step + width].astype(
            jnp.float32
        )
        total = total + kernel[:, tap_index][:, None, None] * window
    return total


def normal_cdf(values):
    return 0.5 * (1.0 + lax.erf(values * ROOT_HALF))


def gelu_slope(values):
    return normal_cdf(values) + values * jnp.exp(-0.5 * values * values) * DENSITY_SCALE


def encoder_forward(padded, enc_params):
    dw_weight, dw_bias, norm_gain, norm_bias, w_in, b_in, w_out, b_out, layer_scale = enc_params
    height = padded.shape[1] - 6
    width = padded.shape[2] - 6
    conv = depthwise(padded, dw_weight, height, width, False) + dw_bias[:, None, None]
    centre = conv - jnp.mean(conv, axis=0, keepdims=True)
    inv_std = lax.rsqrt(jnp.mean(centre * centre, axis=0, keepdims=True) + EPSILON)
    scaled = centre * inv_std
    normed = (scaled * norm_gain[:, None, None] + norm_bias[:, None, None]).astype(jnp.bfloat16)
    before = product("chw,cd->dhw", normed, w_in) + b_in[:, None, None]
    active = (before * normal_cdf(before)).astype(jnp.bfloat16)
    branch = product("dhw,dc->chw", active, w_out) + b_out[:, None, None]
    inner = padded[:, 3 : 3 + height, 3 : 3 + width].astype(jnp.float32)
    output = (inner + layer_scale[:, None, None] * branch).astype(jnp.bfloat16)
    return (output, (scaled, inv_std, normed, before, active, branch))


def encoder_backward(saved, grad_out, enc_params):
    dw_weight, dw_bias, norm_gain, norm_bias, w_in, b_in, w_out, b_out, layer_scale = enc_params
    scaled, inv_std, normed, before, active, branch = saved
    grad_float = grad_out.astype(jnp.float32)
    layerscale_grad = jnp.sum(branch * grad_float, axis=(1, 2))
    d_branch = (layer_scale[:, None, None] * grad_float).astype(jnp.bfloat16)
    projbias_grad = jnp.sum(d_branch.astype(jnp.float32), axis=(1, 2))
    project_grad = product("dhw,chw->dc", active, d_branch)
    d_active = product("chw,dc->dhw", d_branch, w_out)
    d_before = (d_active * gelu_slope(before)).astype(jnp.bfloat16)
    expbias_grad = jnp.sum(d_before.astype(jnp.float32), axis=(1, 2))
    expand_grad = product("chw,dhw->cd", normed, d_before)
    d_normed = product("dhw,cd->chw", d_before, w_in)
    gain_grad = jnp.sum(d_normed * scaled, axis=(1, 2))
    normbias_grad = jnp.sum(d_normed, axis=(1, 2))
    d_scaled = d_normed * norm_gain[:, None, None]
    d_conv = inv_std * (
        d_scaled
        - jnp.mean(d_scaled, axis=0, keepdims=True)
        - scaled * jnp.mean(d_scaled * scaled, axis=0, keepdims=True)
    )
    grads = (
        gain_grad,
        normbias_grad,
        expand_grad,
        expbias_grad,
        project_grad,
        projbias_grad,
        layerscale_grad,
    )
    return (d_conv.astype(jnp.bfloat16), grads)


def conv_backward(padded, d_conv, d_padded, grad_out, dw_weight):
    height = d_conv.shape[1]
    width = d_conv.shape[2]
    d_input = grad_out.astype(jnp.float32) + depthwise(d_padded, dw_weight, height, width, True)
    conv_float = d_conv.astype(jnp.float32)
    columns = []
    for tap_index in range(49):
        down_step = tap_index // 7
        side_step = tap_index % 7
        window = padded[:, down_step : down_step + height, side_step : side_step + width].astype(
            jnp.float32
        )
        columns.append(jnp.sum(window * conv_float, axis=(1, 2)))
    kernel_grad = jnp.stack(columns, axis=1)
    convbias_grad = jnp.sum(conv_float, axis=(1, 2))
    return (d_input, kernel_grad, convbias_grad)


def decoder(encoded, label_tile, w_lateral, b_lateral, w_class, b_class):
    lateral_pre = product("chw,cl->lhw", encoded, w_lateral) + b_lateral[:, None, None]
    lateral = (lateral_pre * normal_cdf(lateral_pre)).astype(jnp.bfloat16)
    logits = product("lhw,lk->khw", lateral, w_class) + b_class[:, None, None]
    highest = jnp.max(logits, axis=0, keepdims=True)
    shifted = logits - highest
    totals = jnp.sum(jnp.exp(shifted), axis=0, keepdims=True)
    log_total = highest + jnp.log(totals)
    classes = jnp.arange(logits.shape[0], dtype=jnp.int32)
    onehot = (label_tile[None, :, :] == classes[:, None, None]).astype(jnp.float32)
    loss_sum = jnp.sum(log_total[0] - jnp.sum(onehot * logits, axis=0))
    d_logits = (jnp.exp(shifted) / totals - onehot).astype(jnp.bfloat16)
    classify_grad = product("lhw,khw->lk", lateral, d_logits)
    clsbias_grad = jnp.sum(d_logits.astype(jnp.float32), axis=(1, 2))
    d_lateral_raw = product("khw,lk->lhw", d_logits, w_class)
    d_lateral = (d_lateral_raw * gelu_slope(lateral_pre)).astype(jnp.bfloat16)
    lateral_grad = product("chw,lhw->cl", encoded, d_lateral)
    latbias_grad = jnp.sum(d_lateral.astype(jnp.float32), axis=(1, 2))
    d_encoded = product("lhw,cl->chw", d_lateral, w_lateral).astype(jnp.bfloat16)
    return (d_encoded, loss_sum, (lateral_grad, latbias_grad, classify_grad, clsbias_grad))


LANES = 128


def tile_order(x):
    rows, cols = x.shape
    x = x.reshape(rows // 8, 8, cols // LANES, LANES).transpose(0, 2, 1, 3)
    return x.reshape(rows * cols // LANES, LANES)


def from_tile_order(x, shape):
    rows, cols = shape
    x = x.reshape(rows // 8, cols // LANES, 8, LANES).transpose(0, 2, 1, 3)
    return x.reshape(rows, cols)


def tiled(shape):
    return len(shape) == 2 and shape[0] % 8 == 0 and shape[1] % LANES == 0


def pack_rows(parts, multiple):
    shapes, rows = [], []
    for part in parts:
        shapes.append(part.shape)
        if tiled(part.shape):
            rows.append(tile_order(part))
            continue
        flat = part.reshape(-1)
        size = flat.shape[0]
        padded_rows = -(-size // (8 * LANES)) * 8
        flat = jnp.pad(flat, (0, padded_rows * LANES - size))
        rows.append(flat.reshape(padded_rows, LANES))
    total = sum(r.shape[0] for r in rows)
    extra = -total % multiple
    if extra:
        rows.append(jnp.zeros((extra, LANES), jnp.float32))
    return jnp.concatenate(rows, axis=0), shapes


def unpack_rows(buffer, shapes):
    out, at = [], 0
    for shape in shapes:
        size = math.prod(shape)
        padded_rows = -(-size // (8 * LANES)) * 8
        piece = buffer[at : at + padded_rows]
        if tiled(shape):
            out.append(from_tile_order(piece, shape))
        else:
            out.append(piece.reshape(-1)[:size].reshape(shape))
        at += padded_rows
    return out


def spread(value, bits):
    out = 0
    for k, bit_at in enumerate(bits):
        if (value >> k) & 1:
            out |= 1 << bit_at
    return out


def butterfly_psum(buffer, axes, stages, scale_of, ties):
    index = lax.axis_index(axes)
    count = math.prod(lax.axis_size(a) for a in axes)
    offset = jnp.zeros((), jnp.int32)
    places = []
    for bits in stages:
        ways = 1 << len(bits)
        mine = sum(((index >> bit_at) & 1) << k for k, bit_at in enumerate(bits))
        pieces = buffer.reshape(ways, buffer.shape[0] // ways, buffer.shape[1])
        total = lax.dynamic_index_in_dim(pieces, mine, 0, keepdims=False)
        for step in range(1, ways):
            flip = spread(step, bits)
            pairs = [(i, i ^ flip) for i in range(count)]
            send = lax.dynamic_index_in_dim(pieces, mine ^ step, 0, keepdims=False)
            total = total + lax.ppermute(send, axes, pairs)
        offset = offset * ways + mine
        places.append((bits, mine))
        buffer = total
        if len(places) in ties:
            buffer, ties[len(places)] = lax.optimization_barrier((buffer, ties[len(places)]))
    rows = buffer.shape[0]
    position = (offset * rows + lax.broadcasted_iota(jnp.int32, buffer.shape, 0)) * buffer.shape[1]
    position = position + lax.broadcasted_iota(jnp.int32, buffer.shape, 1)
    buffer = buffer * scale_of(position)
    for bits, mine in reversed(places):
        ways = 1 << len(bits)
        both = jnp.zeros((ways,) + buffer.shape, buffer.dtype)
        both = lax.dynamic_update_index_in_dim(both, buffer, mine, 0)
        for step in range(1, ways):
            flip = spread(step, bits)
            pairs = [(i, i ^ flip) for i in range(count)]
            other = lax.ppermute(buffer, axes, pairs)
            both = lax.dynamic_update_index_in_dim(both, other, mine ^ step, 0)
        buffer = both.reshape(-1, buffer.shape[1])
    return buffer, ties


def shards(
    features,
    labels,
    dw_weight,
    dw_bias,
    norm_gain,
    norm_bias,
    w_in,
    b_in,
    w_out,
    b_out,
    layer_scale,
    w_lateral,
    b_lateral,
    w_class,
    b_class,
):
    enc_params = (dw_weight, dw_bias, norm_gain, norm_bias, w_in, b_in, w_out, b_out, layer_scale)
    section = lax.axis_index("section")
    micro_count = features.shape[0]
    height = features.shape[2]
    width = features.shape[3]
    axes = ("section", "row", "col")

    def rimmed(tile):
        return padded_2(tile, (("row", 1), ("col", 2)), 3)

    tile = lax.dynamic_index_in_dim(features, section, 0, keepdims=False)
    label_tile = lax.dynamic_index_in_dim(labels, section, 0, keepdims=False)
    padded = rimmed(tile)
    output, saved = encoder_forward(padded, enc_params)
    returned, loss_sum, dec_grads = decoder(output, label_tile, w_lateral, b_lateral, w_class, b_class)
    d_conv, enc_grads = encoder_backward(saved, returned, enc_params)
    d_padded = rimmed(d_conv)
    d_input, kernel_grad, convbias_grad = conv_backward(padded, d_conv, d_padded, returned, dw_weight)
    (
        gain_grad,
        normbias_grad,
        expand_grad,
        expbias_grad,
        project_grad,
        projbias_grad,
        layerscale_grad,
    ) = enc_grads
    lateral_grad, latbias_grad, classify_grad, clsbias_grad = dec_grads
    vectors = [convbias_grad, gain_grad, normbias_grad, expbias_grad, projbias_grad]
    vectors += [layerscale_grad, latbias_grad, clsbias_grad, loss_sum.reshape(1)]
    joined = jnp.concatenate(vectors)
    parts = [joined, kernel_grad, expand_grad, project_grad.T, lateral_grad, classify_grad]
    count = math.prod(lax.axis_size(a) for a in axes)
    buffer, shapes = pack_rows(parts, count * 2)
    cell_count = micro_count * height * width * lax.axis_size("row") * lax.axis_size("col")
    grad_scale = 1.0 / math.sqrt(cell_count)
    loss_at = joined.shape[0] - 1

    def scale_of(position):
        return jnp.where(position == loss_at, 1.0 / cell_count, grad_scale).astype(jnp.float32)

    half = d_conv.shape[0] * 2 // 3

    def input_part(low, high):
        flipped = depthwise(d_padded[low:high], dw_weight[low:high], height, width, True)
        return returned[low:high].astype(jnp.float32) + flipped

    ties = {2: input_part(0, half), 3: input_part(half, d_conv.shape[0])}
    buffer, ties = butterfly_psum(buffer, axes, [(3,), (6, 0), (1, 2), (4, 5)], scale_of, ties)
    d_input = jnp.concatenate([ties[2], ties[3]], axis=0)
    joined, kernel_grad, expand_grad, project_grad, lateral_grad, classify_grad = unpack_rows(
        buffer, shapes
    )
    project_grad = project_grad.T
    sizes = [v.shape[0] for v in vectors]
    cuts = [sum(sizes[:k]) for k in range(len(sizes) + 1)]
    (
        convbias_grad,
        gain_grad,
        normbias_grad,
        expbias_grad,
        projbias_grad,
        layerscale_grad,
        latbias_grad,
        clsbias_grad,
        loss_total,
    ) = [joined[cuts[k] : cuts[k + 1]] for k in range(len(sizes))]
    return (
        d_input[None],
        loss_total[0],
        kernel_grad,
        convbias_grad,
        gain_grad,
        normbias_grad,
        expand_grad,
        expbias_grad,
        project_grad,
        projbias_grad,
        layerscale_grad,
        lateral_grad,
        latbias_grad,
        classify_grad,
        clsbias_grad,
    )


def solution(mesh):
    placed = (
        P(None, None, "row", "col"),
        P(None, "row", "col"),
        P(),
        P(),
        P(),
        P(),
        P(),
        P(),
        P(),
        P(),
        P(),
        P(),
        P(),
        P(),
        P(),
    )
    return jax.shard_map(
        shards,
        mesh=mesh,
        in_specs=placed,
        out_specs=(
            P("section", None, "row", "col"),
            P(),
            P(),
            P(),
            P(),
            P(),
            P(),
            P(),
            P(),
            P(),
            P(),
            P(),
            P(),
            P(),
            P(),
        ),
        check_vma=False,
    )
```
